32 devices in a mesh: seq: 8 (over z, x), win: 4 (over y, core).
Axes of the slice: x: 2, y: 2, z: 4, core: 2. Of those that a mesh axis runs over, the one named last changes fastest.
Arguments:
- inputs: bfloat16 [4, 3072, 1536], P('win', 'seq'), may hold values from -6 to 6
- cotangent: bfloat16 [4, 3072, 1536], P('win', 'seq'), may hold values from -6 to 6
- w_dilated: bfloat16 [2, 1536, 3, 768], P(None, ('seq', 'win')), may hold values from -0.09375 to 0.09375
- w_mix: bfloat16 [2, 1536, 768], P(None, ('seq', 'win')), may hold values from -0.21875 to 0.21875
- in_scale: float32 [2, 1536], replicated, may hold values from 0.1 to 1.9
- in_shift: float32 [2, 1536], replicated, may hold values from -3 to 3
- mid_scale: float32 [2, 768], replicated, may hold values from 0.1 to 1.9
- mid_shift: float32 [2, 768], replicated, may hold values from -3 to 3
Outputs:
- output: bfloat16 [4, 3072, 1536], P('win', 'seq')
- input_gradient: float32 [4, 3072, 1536], P('win', 'seq')
- dilated_weight_gradient: float32 [2, 1536, 3, 768], P(None, ('seq', 'win'))
- grad_mix: float32 [2, 1536, 768], P(None, ('seq', 'win'))
The draws below stay inside these ranges and needn't reach their ends.
All inputs are finite; a program needn't handle non-finite values.
Results may differ from the reference program's by a relative error of at most 0.034.
Values may be sent and summed in bfloat16 or wider, within the bound.
No kernel may reach another device: no remote copies, remote signals or barrier semaphores. Data moves between devices by JAX's collectives and lax.ppermute only.
A program may use at most 192 MiB of HBM per device.

```python
import math
import jax
import jax.numpy as jnp
from jax import lax

C = 1536
C2 = 768
BLOCKS = 2
P_DEV = 384
LENGTH = 3072
WINDOWS = 4
N_SEQ = 8


def spiked(drawn, stream_key, source, target, shards_of, factor):
    def block_of(axis_at):
        return (jnp.arange(drawn.shape[axis_at]) // (drawn.shape[axis_at] // shards_of)).reshape((-1,) + (1,) * (drawn.ndim - 1 - axis_at))

    one_side = jax.random.permutation(stream_key, shards_of)[block_of(target)]
    other_side = (block_of(target) + shards_of // 2) % shards_of
    return jnp.where((block_of(source) == one_side) | (block_of(source) == other_side), factor * drawn, drawn)


def block_scale(key, dims, split, least, top_value):
    level, own = 1.0, jax.random.fold_in(key, 6)
    for dim, shards_of in split:
        heights = jnp.exp(jax.random.uniform(jax.random.fold_in(own, dim), (shards_of,), jnp.float32, least / len(split), top_value / len(split)))
        level = level * jnp.repeat(heights, dims[dim] // shards_of).reshape([-1 if axis == dim else 1 for axis in range(len(dims))])
    return level


def bell_draw(key, shape, deviation, most, pieces=(), kind=jnp.bfloat16):
    values = deviation * jax.random.normal(key, shape, jnp.float32)
    if pieces:
        values = values * block_scale(key, shape, pieces, -0.22, 0.18)
    return jnp.clip(values, -most, most).astype(kind)


def gaussian_with(key, shape, spread, limit, shards, heavy, kind=jnp.bfloat16):
    values = spread * jax.random.normal(key, shape, jnp.float32)
    if shards:
        values = values * block_scale(key, shape, shards, -0.22, 0.18)
    return jnp.clip(spiked(values, jax.random.fold_in(key, 3), *heavy), -limit, limit).astype(kind)


def setup_inputs(seed: int = 0) -> dict:
    arg_keys = jax.random.split(jax.random.key(seed), 9)
    inputs = gaussian_with(arg_keys[0], (WINDOWS, LENGTH, C), 1.0, 6.0, ((0, 4), (1, 8)), (1, 2, 8, 2.0))
    cotangent = gaussian_with(arg_keys[1], (WINDOWS, LENGTH, C), 1.0, 6.0, ((0, 4), (1, 8)), (1, 2, 8, 2.0))
    w_dilated = bell_draw(arg_keys[2], (BLOCKS, C, 3, C2), (3 * C) ** -0.5, 0.09375, ((1, 32),))
    w_mix = bell_draw(arg_keys[3], (BLOCKS, C, C2), C2 ** -0.5, 0.21875, ((1, 32),))
    in_scale = jnp.clip(1.0 + 0.18 * jax.random.normal(arg_keys[4], (BLOCKS, C), jnp.float32), 0.1, 1.9)
    in_shift = bell_draw(arg_keys[5], (BLOCKS, C), 0.5, 3.0, (), jnp.float32)
    mid_scale = jnp.clip(1.0 + 0.18 * jax.random.normal(arg_keys[6], (BLOCKS, C2), jnp.float32), 0.1, 1.9)
    mid_shift = bell_draw(arg_keys[7], (BLOCKS, C2), 0.5, 3.0, (), jnp.float32)
    return {"inputs": inputs, "cotangent": cotangent, "w_dilated": w_dilated, "w_mix": w_mix, "in_scale": in_scale, "in_shift": in_shift, "mid_scale": mid_scale, "mid_shift": mid_shift}


dilation_steps = (8, 16)

def gelu_value(values):
    return jax.nn.gelu(values, approximate=True)

def gelu_back(pre_values, upstream_gradient):
    return jax.vjp(gelu_value, pre_values)[1](upstream_gradient)[0]

def rounded_values(values):
    return lax.optimization_barrier(values.astype(jnp.bfloat16)).astype(jnp.float32)

def reference(inputs, cotangent, w_dilated, w_mix, in_scale, in_shift, mid_scale, mid_shift):
    window_len = inputs.shape[1]
    inverse_square_root = 1.0 / math.sqrt(inputs.shape[0] * window_len)
    seq_ids = jnp.arange(N_SEQ, dtype=jnp.int32)
    residual_block_count = len(dilation_steps)

    def single_window_rows(pair):
        x_window, cot_window = pair
        stream = x_window.astype(jnp.float32)
        saved = []
        for residual_block_index in range(residual_block_count):
            dilation = dilation_steps[residual_block_index]
            pre_in = stream * in_scale[residual_block_index] + in_shift[residual_block_index]
            activated = gelu_value(pre_in).astype(jnp.bfloat16)
            padded = jnp.pad(activated, ((dilation, dilation), (0, 0)))
            hidden = jnp.zeros((window_len, C2), jnp.float32)
            for kernel_tap in range(3):
                lower = kernel_tap * dilation
                hidden = hidden + jnp.dot(padded[lower:lower + window_len], w_dilated[residual_block_index][:, kernel_tap, :], preferred_element_type=jnp.float32)
            pre_mid = hidden * mid_scale[residual_block_index] + mid_shift[residual_block_index]
            middle = gelu_value(pre_mid).astype(jnp.bfloat16)
            stream = stream + jnp.dot(middle, w_mix[residual_block_index].T, preferred_element_type=jnp.float32)
            saved.append((pre_in, padded, pre_mid, middle))
        output = stream.astype(jnp.bfloat16)
        upstream_gradient = cot_window.astype(jnp.float32)
        dilated_gradient_sums = [None] * residual_block_count
        mixing_gradient_sums = [None] * residual_block_count
        for residual_block_index in reversed(range(residual_block_count)):
            dilation = dilation_steps[residual_block_index]
            pre_in, padded, pre_mid, middle = saved[residual_block_index]
            cot_here = upstream_gradient.astype(jnp.bfloat16)
            d_mid = jnp.dot(cot_here, w_mix[residual_block_index], preferred_element_type=jnp.float32)
            d_hidden = (gelu_back(pre_mid, d_mid) * mid_scale[residual_block_index]).astype(jnp.bfloat16)
            d_pad = jnp.pad(d_hidden, ((dilation, dilation), (0, 0)))
            d_act = jnp.zeros((window_len, C), jnp.float32)
            for kernel_tap in range(3):
                lower = (2 - kernel_tap) * dilation
                d_act = d_act + jnp.dot(d_pad[lower:lower + window_len], w_dilated[residual_block_index][:, kernel_tap, :].T, preferred_element_type=jnp.float32)

            def add_block(loop_carry, seq_id):
                begin = seq_id * P_DEV
                grad_piece = lax.dynamic_slice_in_dim(d_hidden, begin, P_DEV, 0).astype(jnp.float32)
                cot_piece = lax.dynamic_slice_in_dim(cot_here, begin, P_DEV, 0).astype(jnp.float32)
                mid_piece = lax.dynamic_slice_in_dim(middle, begin, P_DEV, 0).astype(jnp.float32)
                kernel_taps = []
                for kernel_tap in range(3):
                    act_piece = lax.dynamic_slice_in_dim(padded, begin + kernel_tap * dilation, P_DEV, 0).astype(jnp.float32)
                    kernel_taps.append(jnp.einsum('pc,pe->ce', act_piece, grad_piece))
                dilated_gradient_term = jnp.stack(kernel_taps, axis=1) * inverse_square_root
                mixing_gradient_term = jnp.einsum('pc,pe->ce', cot_piece, mid_piece) * inverse_square_root
                return ((loop_carry[0] + rounded_values(dilated_gradient_term), loop_carry[1] + rounded_values(mixing_gradient_term)), None)
            start_sums = (jnp.zeros((C, 3, C2), jnp.float32), jnp.zeros((C, C2), jnp.float32))
            gradient_totals, unused = lax.scan(add_block, start_sums, seq_ids)
            dilated_gradient_sums[residual_block_index] = gradient_totals[0].astype(jnp.bfloat16)
            mixing_gradient_sums[residual_block_index] = gradient_totals[1].astype(jnp.bfloat16)
            upstream_gradient = upstream_gradient + gelu_back(pre_in, d_act) * in_scale[residual_block_index]
        return (output, upstream_gradient, jnp.stack(dilated_gradient_sums), jnp.stack(mixing_gradient_sums))
    output, input_gradient, dilated_weight_stack, mixing_weight_stack = lax.map(single_window_rows, (inputs, cotangent))
    dilated_weight_gradient = lax.optimization_barrier(jnp.sum(dilated_weight_stack.astype(jnp.float32), axis=0))
    grad_mix = lax.optimization_barrier(jnp.sum(mixing_weight_stack.astype(jnp.float32), axis=0))
    return (output, input_gradient, dilated_weight_gradient, grad_mix)
```

```python
import math

import jax
import jax.numpy as jnp
from jax import lax
from jax.sharding import PartitionSpec as P

dilation_steps = (8, 16)


def padded_2(block, sides, width):
    for axis, dim in sides:
        count = lax.axis_size(axis)
        forward = [(i, i + 1) for i in range(count - 1)]
        backward = [(target, source) for source, target in forward]
        low = lax.ppermute(
            lax.slice_in_dim(block, block.shape[dim] - width, None, axis=dim), axis, forward
        )
        high = lax.ppermute(lax.slice_in_dim(block, 0, width, axis=dim), axis, backward)
        block = jnp.concatenate([low, block, high], axis=dim)
    return block


def gelu_value(values):
    return jax.nn.gelu(values, approximate=True)


def gelu_back(pre_values, upstream_gradient):
    return jax.vjp(gelu_value, pre_values)[1](upstream_gradient)[0]


def dilated_conv(padded, w_conv, dilation, out_rows):
    hidden = jnp.dot(padded[0:out_rows], w_conv[:, 0, :], preferred_element_type=jnp.float32)
    for kernel_tap in (1, 2):
        lower = kernel_tap * dilation
        hidden = hidden + jnp.dot(
            padded[lower : lower + out_rows],
            w_conv[:, kernel_tap, :],
            preferred_element_type=jnp.float32,
        )
    return hidden


def fetch_weights(w_dilated, w_mix):
    blocks, rows, taps, c2 = w_dilated.shape
    local = jnp.concatenate(
        [w_dilated.reshape(blocks, rows, taps * c2).transpose(1, 0, 2).reshape(rows, -1),
         w_mix.transpose(1, 0, 2).reshape(rows, -1)],
        axis=1,
    )
    gathered = lax.all_gather(local, ("seq", "win"), axis=0, tiled=True)
    full_rows = gathered.shape[0]
    split = blocks * taps * c2
    return [
        (
            gathered[:, b * taps * c2 : (b + 1) * taps * c2].reshape(full_rows, taps, c2),
            gathered[:, split + b * c2 : split + (b + 1) * c2],
        )
        for b in range(blocks)
    ]


def weight_gradient_terms(padded, d_hidden, cot_here, middle, dilation, inverse_square_root):
    row_count = d_hidden.shape[0]
    kernel_taps = [
        jnp.einsum(
            "pc,pe->ce",
            padded[kernel_tap * dilation : kernel_tap * dilation + row_count],
            d_hidden,
            preferred_element_type=jnp.float32,
        )
        for kernel_tap in range(3)
    ]
    dilated = (jnp.concatenate(kernel_taps, axis=1) * inverse_square_root).astype(jnp.bfloat16)
    mixed = (
        jnp.einsum("pc,pe->ce", cot_here, middle, preferred_element_type=jnp.float32)
        * inverse_square_root
    ).astype(jnp.bfloat16)
    return dilated, mixed


def per_device(inputs, cotangent, w_dilated, w_mix, in_scale, in_shift, mid_scale, mid_shift):
    x_local = inputs[0]
    cot_local = cotangent[0]
    row_count = x_local.shape[0]
    window_len = lax.axis_size("seq") * row_count
    inverse_square_root = 1.0 / math.sqrt(lax.axis_size("win") * inputs.shape[0] * window_len)
    residual_block_count = len(dilation_steps)
    saved = []
    weights = fetch_weights(w_dilated, w_mix)
    stream = x_local.astype(jnp.float32)
    for residual_block_index in range(residual_block_count):
        dilation = dilation_steps[residual_block_index]
        w_conv, w_out = weights[residual_block_index]
        pre_in = stream * in_scale[residual_block_index] + in_shift[residual_block_index]
        activated = gelu_value(pre_in).astype(jnp.bfloat16)
        padded = padded_2(activated, (("seq", 0),), dilation)
        pre_mid = (
            dilated_conv(padded, w_conv, dilation, row_count) * mid_scale[residual_block_index]
            + mid_shift[residual_block_index]
        )
        middle = gelu_value(pre_mid).astype(jnp.bfloat16)
        stream = stream + jnp.einsum("pe,ce->pc", middle, w_out, preferred_element_type=jnp.float32)
        saved.append((w_conv, w_out, pre_in, padded, pre_mid, middle))
    output = stream.astype(jnp.bfloat16)
    upstream_gradient = cot_local.astype(jnp.float32)
    dilated_weight_gradients = [None] * residual_block_count
    mixing_weight_gradients = [None] * residual_block_count
    for residual_block_index in reversed(range(residual_block_count)):
        dilation = dilation_steps[residual_block_index]
        w_conv, w_out, pre_in, padded, pre_mid, middle = saved[residual_block_index]
        cot_here = upstream_gradient.astype(jnp.bfloat16)
        d_mid = jnp.dot(cot_here, w_out, preferred_element_type=jnp.float32)
        d_hidden = (gelu_back(pre_mid, d_mid) * mid_scale[residual_block_index]).astype(
            jnp.bfloat16
        )
        d_pad = padded_2(d_hidden, (("seq", 0),), dilation)
        d_act = jnp.einsum(
            "pe,ce->pc",
            d_pad[2 * dilation : 2 * dilation + row_count],
            w_conv[:, 0, :],
            preferred_element_type=jnp.float32,
        )
        for kernel_tap in (1, 2):
            lower = (2 - kernel_tap) * dilation
            d_act = d_act + jnp.einsum(
                "pe,ce->pc",
                d_pad[lower : lower + row_count],
                w_conv[:, kernel_tap, :],
                preferred_element_type=jnp.float32,
            )
        (
            dilated_weight_gradients[residual_block_index],
            mixing_weight_gradients[residual_block_index],
        ) = weight_gradient_terms(padded, d_hidden, cot_here, middle, dilation, inverse_square_root)
        upstream_gradient = (
            upstream_gradient + gelu_back(pre_in, d_act) * in_scale[residual_block_index]
        )
    summed = lax.psum_scatter(
        jnp.concatenate(dilated_weight_gradients + mixing_weight_gradients, axis=1),
        ("seq", "win"),
        scatter_dimension=0,
        tiled=True,
    ).astype(jnp.float32)
    own_rows = summed.shape[0]
    taps, c2 = w_dilated.shape[2], w_dilated.shape[3]
    split = residual_block_count * taps * c2
    return (
        output[None],
        upstream_gradient[None],
        summed[:, :split].reshape(own_rows, residual_block_count, taps, c2).transpose(1, 0, 2, 3),
        summed[:, split:].reshape(own_rows, residual_block_count, c2).transpose(1, 0, 2),
    )


def solution(mesh):
    in_specs = (
        P("win", "seq", None),
        P("win", "seq", None),
        P(None, ("seq", "win"), None, None),
        P(None, ("seq", "win"), None),
        P(),
        P(),
        P(),
        P(),
    )
    out_specs = (
        P("win", "seq", None),
        P("win", "seq", None),
        P(None, ("seq", "win"), None, None),
        P(None, ("seq", "win"), None),
    )
    return jax.shard_map(
        per_device, mesh=mesh, in_specs=in_specs, out_specs=out_specs, check_vma=False
    )
```

```python
import math

import jax
import jax.numpy as jnp
from jax import lax
from jax.experimental import pallas as pl
from jax.sharding import PartitionSpec as P

dilation_steps = (8, 16)


def padded_2(block, sides, width):
    for axis, dim in sides:
        count = lax.axis_size(axis)
        forward = [(i, i + 1) for i in range(count - 1)]
        backward = [(target, source) for source, target in forward]
        low = lax.ppermute(
            lax.slice_in_dim(block, block.shape[dim] - width, None, axis=dim), axis, forward
        )
        high = lax.ppermute(lax.slice_in_dim(block, 0, width, axis=dim), axis, backward)
        block = jnp.concatenate([low, block, high], axis=dim)
    return block


def gelu_value(values):
    return jax.nn.gelu(values, approximate=True)


def gelu_back(pre_values, upstream_gradient):
    return jax.vjp(gelu_value, pre_values)[1](upstream_gradient)[0]


def dilated_conv(padded, w_conv, dilation, out_rows):
    hidden = jnp.dot(padded[0:out_rows], w_conv[:, 0, :], preferred_element_type=jnp.float32)
    for kernel_tap in (1, 2):
        lower = kernel_tap * dilation
        hidden = hidden + jnp.dot(
            padded[lower : lower + out_rows],
            w_conv[:, kernel_tap, :],
            preferred_element_type=jnp.float32,
        )
    return hidden


def fetch_weights(w_dilated, w_mix):
    blocks, rows, taps, c2 = w_dilated.shape
    local = jnp.concatenate(
        [w_dilated.reshape(blocks, rows, taps * c2).transpose(1, 0, 2).reshape(rows, -1),
         w_mix.transpose(1, 0, 2).reshape(rows, -1)],
        axis=1,
    )
    gathered = lax.all_gather(local, ("seq", "win"), axis=0, tiled=True)
    full_rows = gathered.shape[0]
    split = blocks * taps * c2
    return [
        (
            gathered[:, b * taps * c2 : (b + 1) * taps * c2].reshape(full_rows, taps, c2),
            gathered[:, split + b * c2 : split + (b + 1) * c2],
        )
        for b in range(blocks)
    ]


def shifted_taps(d_hidden, dilation):
    return jnp.concatenate(
        [jnp.pad(d_hidden, ((k * dilation, (2 - k) * dilation), (0, 0))) for k in range(3)], axis=1
    )


def gradient_kernel(scale, widths, *refs):
    out_ref = refs[-1]
    start = 0
    for pair in range(len(widths)):
        lhs = refs[2 * pair][...]
        rhs = refs[2 * pair + 1][...]
        term = jnp.dot(lhs, rhs, preferred_element_type=jnp.float32) * scale
        out_ref[:, start : start + widths[pair]] = term.astype(out_ref.dtype)
        start += widths[pair]


def weight_gradient_buffer(pairs, inverse_square_root, row_tile=256):
    rows = pairs[0][0].shape[0]
    widths = tuple(rhs.shape[1] for _, rhs in pairs)
    in_specs = []
    operands = []
    for lhs, rhs in pairs:
        in_specs.append(pl.BlockSpec((row_tile, lhs.shape[1]), lambda i: (i, 0)))
        in_specs.append(pl.BlockSpec(rhs.shape, lambda i: (0, 0)))
        operands += [lhs, rhs]
    return pl.pallas_call(
        lambda *refs: gradient_kernel(inverse_square_root, widths, *refs),
        grid=(rows // row_tile,),
        in_specs=in_specs,
        out_specs=pl.BlockSpec((row_tile, sum(widths)), lambda i: (i, 0)),
        out_shape=jax.ShapeDtypeStruct((rows, sum(widths)), jnp.bfloat16),
    )(*operands)


def per_device(inputs, cotangent, w_dilated, w_mix, in_scale, in_shift, mid_scale, mid_shift):
    x_local = inputs[0]
    cot_local = cotangent[0]
    row_count = x_local.shape[0]
    window_len = lax.axis_size("seq") * row_count
    inverse_square_root = 1.0 / math.sqrt(lax.axis_size("win") * inputs.shape[0] * window_len)
    residual_block_count = len(dilation_steps)
    saved = []
    weights = fetch_weights(w_dilated, w_mix)
    stream = x_local.astype(jnp.float32)
    for residual_block_index in range(residual_block_count):
        dilation = dilation_steps[residual_block_index]
        w_conv, w_out = weights[residual_block_index]
        pre_in = stream * in_scale[residual_block_index] + in_shift[residual_block_index]
        activated = gelu_value(pre_in).astype(jnp.bfloat16)
        padded = padded_2(activated, (("seq", 0),), dilation)
        pre_mid = (
            dilated_conv(padded, w_conv, dilation, row_count) * mid_scale[residual_block_index]
            + mid_shift[residual_block_index]
        )
        middle = gelu_value(pre_mid).astype(jnp.bfloat16)
        stream = stream + jnp.einsum("pe,ce->pc", middle, w_out, preferred_element_type=jnp.float32)
        saved.append((w_conv, w_out, pre_in, padded, pre_mid, middle))
    output = stream.astype(jnp.bfloat16)
    upstream_gradient = cot_local.astype(jnp.float32)
    dilated_weight_gradients = [None] * residual_block_count
    mixing_weight_gradients = [None] * residual_block_count
    for residual_block_index in reversed(range(residual_block_count)):
        dilation = dilation_steps[residual_block_index]
        w_conv, w_out, pre_in, padded, pre_mid, middle = saved[residual_block_index]
        cot_here = upstream_gradient.astype(jnp.bfloat16)
        d_mid = jnp.dot(cot_here, w_out, preferred_element_type=jnp.float32)
        d_hidden = (gelu_back(pre_mid, d_mid) * mid_scale[residual_block_index]).astype(
            jnp.bfloat16
        )
        d_pad = padded_2(d_hidden, (("seq", 0),), dilation)
        d_act = jnp.einsum(
            "pe,ce->pc",
            d_pad[2 * dilation : 2 * dilation + row_count],
            w_conv[:, 0, :],
            preferred_element_type=jnp.float32,
        )
        for kernel_tap in (1, 2):
            lower = (2 - kernel_tap) * dilation
            d_act = d_act + jnp.einsum(
                "pe,ce->pc",
                d_pad[lower : lower + row_count],
                w_conv[:, kernel_tap, :],
                preferred_element_type=jnp.float32,
            )
        dilated_weight_gradients[residual_block_index] = (padded.T, shifted_taps(d_hidden, dilation))
        mixing_weight_gradients[residual_block_index] = (cot_here.T, middle)
        upstream_gradient = (
            upstream_gradient + gelu_back(pre_in, d_act) * in_scale[residual_block_index]
        )
    summed = lax.psum_scatter(
        weight_gradient_buffer(dilated_weight_gradients + mixing_weight_gradients, inverse_square_root),
        ("seq", "win"),
        scatter_dimension=0,
        tiled=True,
    ).astype(jnp.float32)
    own_rows = summed.shape[0]
    taps, c2 = w_dilated.shape[2], w_dilated.shape[3]
    split = residual_block_count * taps * c2
    return (
        output[None],
        upstream_gradient[None],
        summed[:, :split].reshape(own_rows, residual_block_count, taps, c2).transpose(1, 0, 2, 3),
        summed[:, split:].reshape(own_rows, residual_block_count, c2).transpose(1, 0, 2),
    )


def solution(mesh):
    in_specs = (
        P("win", "seq", None),
        P("win", "seq", None),
        P(None, ("seq", "win"), None, None),
        P(None, ("seq", "win"), None),
        P(),
        P(),
        P(),
        P(),
    )
    out_specs = (
        P("win", "seq", None),
        P("win", "seq", None),
        P(None, ("seq", "win"), None, None),
        P(None, ("seq", "win"), None),
    )
    return jax.shard_map(
        per_device, mesh=mesh, in_specs=in_specs, out_specs=out_specs, check_vma=False
    )
```

```python
import math

import jax
import jax.numpy as jnp
from jax import lax
from jax.experimental import pallas as pl
from jax.sharding import PartitionSpec as P

dilation_steps = (8, 16)


def padded_2(block, sides, width):
    for axis, dim in sides:
        count = lax.axis_size(axis)
        forward = [(i, i + 1) for i in range(count - 1)]
        backward = [(target, source) for source, target in forward]
        low = lax.ppermute(
            lax.slice_in_dim(block, block.shape[dim] - width, None, axis=dim), axis, forward
        )
        high = lax.ppermute(lax.slice_in_dim(block, 0, width, axis=dim), axis, backward)
        block = jnp.concatenate([low, block, high], axis=dim)
    return block


def gelu_value(values):
    return jax.nn.gelu(values, approximate=True)


def gelu_back(pre_values, upstream_gradient):
    return jax.vjp(gelu_value, pre_values)[1](upstream_gradient)[0]


def conv_forward_kernel(dilation, out_rows, act_ref, w_ref, scale_ref, shift_ref, out_ref):
    width = out_ref.shape[1]
    hidden = jnp.dot(act_ref[0:out_rows, :], w_ref[:, 0:width], preferred_element_type=jnp.float32)
    for kernel_tap in (1, 2):
        lower = kernel_tap * dilation
        hidden = hidden + jnp.dot(
            act_ref[lower : lower + out_rows, :],
            w_ref[:, kernel_tap * width : (kernel_tap + 1) * width],
            preferred_element_type=jnp.float32,
        )
    out_ref[...] = hidden * scale_ref[...] + shift_ref[...]


def conv_backward_kernel(dilation, out_rows, grad_ref, w_ref, out_ref):
    width = grad_ref.shape[1]
    numbers = (((1,), (1,)), ((), ()))
    total = None
    for kernel_tap in range(3):
        lower = (2 - kernel_tap) * dilation
        term = lax.dot_general(
            grad_ref[lower : lower + out_rows, :],
            w_ref[:, kernel_tap * width : (kernel_tap + 1) * width],
            numbers,
            preferred_element_type=jnp.float32,
        )
        total = term if total is None else total + term
    out_ref[...] = total


def conv_forward(padded, gathered, block, c2, scale, shift, dilation, out_rows):
    rows = gathered.shape[0]
    return pl.pallas_call(
        lambda *refs: conv_forward_kernel(dilation, out_rows, *refs),
        grid=(1,),
        in_specs=[
            pl.BlockSpec(padded.shape, lambda i: (0, 0)),
            pl.BlockSpec((rows, 3 * c2), lambda i: (0, block)),
            pl.BlockSpec((1, c2), lambda i: (0, 0)),
            pl.BlockSpec((1, c2), lambda i: (0, 0)),
        ],
        out_specs=pl.BlockSpec((out_rows, c2), lambda i: (0, 0)),
        out_shape=jax.ShapeDtypeStruct((out_rows, c2), jnp.float32),
    )(padded, gathered, scale.reshape(1, c2), shift.reshape(1, c2))


def conv_backward(d_pad, gathered, block, c2, dilation, out_rows):
    rows = gathered.shape[0]
    return pl.pallas_call(
        lambda *refs: conv_backward_kernel(dilation, out_rows, *refs),
        grid=(1,),
        in_specs=[
            pl.BlockSpec(d_pad.shape, lambda i: (0, 0)),
            pl.BlockSpec((rows, 3 * c2), lambda i: (0, block)),
        ],
        out_specs=pl.BlockSpec((out_rows, rows), lambda i: (0, 0)),
        out_shape=jax.ShapeDtypeStruct((out_rows, rows), jnp.float32),
    )(d_pad, gathered)


def fetch_weights(w_dilated, w_mix):
    blocks, rows, taps, c2 = w_dilated.shape
    local = jnp.concatenate(
        [w_dilated.reshape(blocks, rows, taps * c2).transpose(1, 0, 2).reshape(rows, -1),
         w_mix.transpose(1, 0, 2).reshape(rows, -1)],
        axis=1,
    )
    gathered = lax.all_gather(local, ("seq", "win"), axis=0, tiled=True)
    split = blocks * taps * c2
    return gathered, [gathered[:, split + b * c2 : split + (b + 1) * c2] for b in range(blocks)]


def shifted_taps(d_hidden, dilation):
    return jnp.concatenate(
        [jnp.pad(d_hidden, ((k * dilation, (2 - k) * dilation), (0, 0))) for k in range(3)], axis=1
    )


def gradient_kernel(scale, widths, *refs):
    out_ref = refs[-1]
    start = 0
    for pair in range(len(widths)):
        lhs = refs[2 * pair][...]
        rhs = refs[2 * pair + 1][...]
        term = jnp.dot(lhs, rhs, preferred_element_type=jnp.float32) * scale
        out_ref[:, start : start + widths[pair]] = term.astype(out_ref.dtype)
        start += widths[pair]


def weight_gradient_buffer(pairs, inverse_square_root, row_tile=256):
    rows = pairs[0][0].shape[0]
    widths = tuple(rhs.shape[1] for _, rhs in pairs)
    in_specs = []
    operands = []
    for lhs, rhs in pairs:
        in_specs.append(pl.BlockSpec((row_tile, lhs.shape[1]), lambda i: (i, 0)))
        in_specs.append(pl.BlockSpec(rhs.shape, lambda i: (0, 0)))
        operands += [lhs, rhs]
    return pl.pallas_call(
        lambda *refs: gradient_kernel(inverse_square_root, widths, *refs),
        grid=(rows // row_tile,),
        in_specs=in_specs,
        out_specs=pl.BlockSpec((row_tile, sum(widths)), lambda i: (i, 0)),
        out_shape=jax.ShapeDtypeStruct((rows, sum(widths)), jnp.bfloat16),
    )(*operands)


def per_device(inputs, cotangent, w_dilated, w_mix, in_scale, in_shift, mid_scale, mid_shift):
    x_local = inputs[0]
    cot_local = cotangent[0]
    row_count = x_local.shape[0]
    window_len = lax.axis_size("seq") * row_count
    inverse_square_root = 1.0 / math.sqrt(lax.axis_size("win") * inputs.shape[0] * window_len)
    residual_block_count = len(dilation_steps)
    saved = []
    gathered, mixing_weights = fetch_weights(w_dilated, w_mix)
    c2 = w_dilated.shape[3]
    stream = x_local.astype(jnp.float32)
    for residual_block_index in range(residual_block_count):
        dilation = dilation_steps[residual_block_index]
        w_out = mixing_weights[residual_block_index]
        pre_in = stream * in_scale[residual_block_index] + in_shift[residual_block_index]
        activated = gelu_value(pre_in).astype(jnp.bfloat16)
        padded = padded_2(activated, (("seq", 0),), dilation)
        pre_mid = conv_forward(
            padded,
            gathered,
            residual_block_index,
            c2,
            mid_scale[residual_block_index],
            mid_shift[residual_block_index],
            dilation,
            row_count,
        )
        middle = gelu_value(pre_mid).astype(jnp.bfloat16)
        stream = stream + jnp.einsum("pe,ce->pc", middle, w_out, preferred_element_type=jnp.float32)
        saved.append((w_out, pre_in, padded, pre_mid, middle))
    output = stream.astype(jnp.bfloat16)
    upstream_gradient = cot_local.astype(jnp.float32)
    dilated_weight_gradients = [None] * residual_block_count
    mixing_weight_gradients = [None] * residual_block_count
    for residual_block_index in reversed(range(residual_block_count)):
        dilation = dilation_steps[residual_block_index]
        w_out, pre_in, padded, pre_mid, middle = saved[residual_block_index]
        cot_here = upstream_gradient.astype(jnp.bfloat16)
        d_mid = jnp.dot(cot_here, w_out, preferred_element_type=jnp.float32)
        d_hidden = (gelu_back(pre_mid, d_mid) * mid_scale[residual_block_index]).astype(
            jnp.bfloat16
        )
        d_pad = padded_2(d_hidden, (("seq", 0),), dilation)
        d_act = conv_backward(d_pad, gathered, residual_block_index, c2, dilation, row_count)
        dilated_weight_gradients[residual_block_index] = (padded.T, shifted_taps(d_hidden, dilation))
        mixing_weight_gradients[residual_block_index] = (cot_here.T, middle)
        upstream_gradient = (
            upstream_gradient + gelu_back(pre_in, d_act) * in_scale[residual_block_index]
        )
    summed = lax.psum_scatter(
        weight_gradient_buffer(dilated_weight_gradients + mixing_weight_gradients, inverse_square_root),
        ("seq", "win"),
        scatter_dimension=0,
        tiled=True,
    ).astype(jnp.float32)
    own_rows = summed.shape[0]
    taps, c2 = w_dilated.shape[2], w_dilated.shape[3]
    split = residual_block_count * taps * c2
    return (
        output[None],
        upstream_gradient[None],
        summed[:, :split].reshape(own_rows, residual_block_count, taps, c2).transpose(1, 0, 2, 3),
        summed[:, split:].reshape(own_rows, residual_block_count, c2).transpose(1, 0, 2),
    )


def solution(mesh):
    in_specs = (
        P("win", "seq", None),
        P("win", "seq", None),
        P(None, ("seq", "win"), None, None),
        P(None, ("seq", "win"), None),
        P(),
        P(),
        P(),
        P(),
    )
    out_specs = (
        P("win", "seq", None),
        P("win", "seq", None),
        P(None, ("seq", "win"), None, None),
        P(None, ("seq", "win"), None),
    )
    return jax.shard_map(
        per_device, mesh=mesh, in_specs=in_specs, out_specs=out_specs, check_vma=False
    )
```

```python
import math

import jax
import jax.numpy as jnp
from jax import lax
from jax.experimental import pallas as pl
from jax.sharding import PartitionSpec as P

dilation_steps = (8, 16)


def padded_2(block, sides, width):
    for axis, dim in sides:
        count = lax.axis_size(axis)
        forward = [(i, i + 1) for i in range(count - 1)]
        backward = [(target, source) for source, target in forward]
        low = lax.ppermute(
            lax.slice_in_dim(block, block.shape[dim] - width, None, axis=dim), axis, forward
        )
        high = lax.ppermute(lax.slice_in_dim(block, 0, width, axis=dim), axis, backward)
        block = jnp.concatenate([low, block, high], axis=dim)
    return block


def gelu_value(values):
    return jax.nn.gelu(values, approximate=True)


def gelu_back(pre_values, upstream_gradient):
    return jax.vjp(gelu_value, pre_values)[1](upstream_gradient)[0]


def conv_forward_kernel(dilation, out_rows, act_ref, w_ref, scale_ref, shift_ref, out_ref):
    width = out_ref.shape[1]
    hidden = jnp.dot(act_ref[0:out_rows, :], w_ref[:, 0:width], preferred_element_type=jnp.float32)
    for kernel_tap in (1, 2):
        lower = kernel_tap * dilation
        hidden = hidden + jnp.dot(
            act_ref[lower : lower + out_rows, :],
            w_ref[:, kernel_tap * width : (kernel_tap + 1) * width],
            preferred_element_type=jnp.float32,
        )
    out_ref[...] = hidden * scale_ref[...] + shift_ref[...]


def conv_backward_kernel(dilation, out_rows, grad_ref, w_ref, out_ref):
    width = grad_ref.shape[1]
    numbers = (((1,), (1,)), ((), ()))
    total = None
    for kernel_tap in range(3):
        lower = (2 - kernel_tap) * dilation
        term = lax.dot_general(
            grad_ref[lower : lower + out_rows, :],
            w_ref[:, kernel_tap * width : (kernel_tap + 1) * width],
            numbers,
            preferred_element_type=jnp.float32,
        )
        total = term if total is None else total + term
    out_ref[...] = total


def conv_forward(padded, gathered, block, c2, scale, shift, dilation, out_rows):
    rows = gathered.shape[0]
    return pl.pallas_call(
        lambda *refs: conv_forward_kernel(dilation, out_rows, *refs),
        grid=(1,),
        in_specs=[
            pl.BlockSpec(padded.shape, lambda i: (0, 0)),
            pl.BlockSpec((rows, 3 * c2), lambda i: (0, block)),
            pl.BlockSpec((1, c2), lambda i: (0, 0)),
            pl.BlockSpec((1, c2), lambda i: (0, 0)),
        ],
        out_specs=pl.BlockSpec((out_rows, c2), lambda i: (0, 0)),
        out_shape=jax.ShapeDtypeStruct((out_rows, c2), jnp.float32),
    )(padded, gathered, scale.reshape(1, c2), shift.reshape(1, c2))


def conv_backward(d_pad, gathered, block, c2, dilation, out_rows):
    rows = gathered.shape[0]
    return pl.pallas_call(
        lambda *refs: conv_backward_kernel(dilation, out_rows, *refs),
        grid=(1,),
        in_specs=[
            pl.BlockSpec(d_pad.shape, lambda i: (0, 0)),
            pl.BlockSpec((rows, 3 * c2), lambda i: (0, block)),
        ],
        out_specs=pl.BlockSpec((out_rows, rows), lambda i: (0, 0)),
        out_shape=jax.ShapeDtypeStruct((out_rows, rows), jnp.float32),
    )(d_pad, gathered)


def fetch_weights(w_dilated, w_mix):
    blocks, rows, taps, c2 = w_dilated.shape
    local = jnp.concatenate(
        [w_dilated.reshape(blocks, rows, taps * c2).transpose(1, 0, 2).reshape(rows, -1),
         w_mix.transpose(1, 0, 2).reshape(rows, -1)],
        axis=1,
    )
    gathered = lax.all_gather(local, ("seq", "win"), axis=0, tiled=True)
    split = blocks * taps * c2
    return gathered, [gathered[:, split + b * c2 : split + (b + 1) * c2] for b in range(blocks)]


def shifted_taps(d_hidden, dilation):
    return jnp.concatenate(
        [jnp.pad(d_hidden, ((k * dilation, (2 - k) * dilation), (0, 0))) for k in range(3)], axis=1
    )


def gradient_kernel(scale, widths, *refs):
    out_ref = refs[-1]
    start = 0
    for pair in range(len(widths)):
        lhs = refs[2 * pair][...]
        rhs = refs[2 * pair + 1][...]
        term = jnp.dot(lhs, rhs, preferred_element_type=jnp.float32) * scale
        out_ref[:, start : start + widths[pair]] = term.astype(out_ref.dtype)
        start += widths[pair]


def weight_gradient_buffer(pairs, inverse_square_root, row_tile=256):
    rows = pairs[0][0].shape[0]
    widths = tuple(rhs.shape[1] for _, rhs in pairs)
    in_specs = []
    operands = []
    for lhs, rhs in pairs:
        in_specs.append(pl.BlockSpec((row_tile, lhs.shape[1]), lambda i: (i, 0)))
        in_specs.append(pl.BlockSpec(rhs.shape, lambda i: (0, 0)))
        operands += [lhs, rhs]
    return pl.pallas_call(
        lambda *refs: gradient_kernel(inverse_square_root, widths, *refs),
        grid=(rows // row_tile,),
        in_specs=in_specs,
        out_specs=pl.BlockSpec((row_tile, sum(widths)), lambda i: (i, 0)),
        out_shape=jax.ShapeDtypeStruct((rows, sum(widths)), jnp.bfloat16),
    )(*operands)


def per_device(inputs, cotangent, w_dilated, w_mix, in_scale, in_shift, mid_scale, mid_shift):
    x_local = inputs[0]
    cot_local = cotangent[0]
    row_count = x_local.shape[0]
    window_len = lax.axis_size("seq") * row_count
    inverse_square_root = 1.0 / math.sqrt(lax.axis_size("win") * inputs.shape[0] * window_len)
    residual_block_count = len(dilation_steps)
    saved = []
    gathered, mixing_weights = fetch_weights(w_dilated, w_mix)
    c2 = w_dilated.shape[3]
    remaining = sum(dilation_steps)
    first_row = lax.axis_index("seq") * row_count
    stream = padded_2(x_local, (("seq", 0),), remaining).astype(jnp.float32)
    for residual_block_index in range(residual_block_count):
        dilation = dilation_steps[residual_block_index]
        w_out = mixing_weights[residual_block_index]
        pre_in = stream * in_scale[residual_block_index] + in_shift[residual_block_index]
        position = first_row - remaining + lax.broadcasted_iota(jnp.int32, (pre_in.shape[0], 1), 0)
        inside = (position >= 0) & (position < window_len)
        activated = jnp.where(inside, gelu_value(pre_in), 0.0).astype(jnp.bfloat16)
        out_rows = row_count + 2 * (remaining - dilation)
        pre_mid = conv_forward(
            activated,
            gathered,
            residual_block_index,
            c2,
            mid_scale[residual_block_index],
            mid_shift[residual_block_index],
            dilation,
            out_rows,
        )
        middle = gelu_value(pre_mid).astype(jnp.bfloat16)
        stream = stream[dilation : dilation + out_rows] + jnp.einsum(
            "pe,ce->pc", middle, w_out, preferred_element_type=jnp.float32
        )
        own = remaining - dilation
        saved.append(
            (
                w_out,
                pre_in[remaining : remaining + row_count],
                activated[own : own + row_count + 2 * dilation],
                pre_mid[own : own + row_count],
                middle[own : own + row_count],
            )
        )
        remaining -= dilation
    output = stream.astype(jnp.bfloat16)
    upstream_gradient = cot_local.astype(jnp.float32)
    dilated_weight_gradients = [None] * residual_block_count
    mixing_weight_gradients = [None] * residual_block_count
    for residual_block_index in reversed(range(residual_block_count)):
        dilation = dilation_steps[residual_block_index]
        w_out, pre_in, padded, pre_mid, middle = saved[residual_block_index]
        cot_here = upstream_gradient.astype(jnp.bfloat16)
        d_mid = jnp.dot(cot_here, w_out, preferred_element_type=jnp.float32)
        d_hidden = (gelu_back(pre_mid, d_mid) * mid_scale[residual_block_index]).astype(
            jnp.bfloat16
        )
        d_pad = padded_2(d_hidden, (("seq", 0),), dilation)
        d_act = conv_backward(d_pad, gathered, residual_block_index, c2, dilation, row_count)
        dilated_weight_gradients[residual_block_index] = (padded.T, shifted_taps(d_hidden, dilation))
        mixing_weight_gradients[residual_block_index] = (cot_here.T, middle)
        upstream_gradient = (
            upstream_gradient + gelu_back(pre_in, d_act) * in_scale[residual_block_index]
        )
    summed = lax.psum_scatter(
        weight_gradient_buffer(dilated_weight_gradients + mixing_weight_gradients, inverse_square_root),
        ("seq", "win"),
        scatter_dimension=0,
        tiled=True,
    ).astype(jnp.float32)
    own_rows = summed.shape[0]
    taps, c2 = w_dilated.shape[2], w_dilated.shape[3]
    split = residual_block_count * taps * c2
    return (
        output[None],
        upstream_gradient[None],
        summed[:, :split].reshape(own_rows, residual_block_count, taps, c2).transpose(1, 0, 2, 3),
        summed[:, split:].reshape(own_rows, residual_block_count, c2).transpose(1, 0, 2),
    )


def solution(mesh):
    in_specs = (
        P("win", "seq", None),
        P("win", "seq", None),
        P(None, ("seq", "win"), None, None),
        P(None, ("seq", "win"), None),
        P(),
        P(),
        P(),
        P(),
    )
    out_specs = (
        P("win", "seq", None),
        P("win", "seq", None),
        P(None, ("seq", "win"), None, None),
        P(None, ("seq", "win"), None),
    )
    return jax.shard_map(
        per_device, mesh=mesh, in_specs=in_specs, out_specs=out_specs, check_vma=False
    )
```

```python
import math

import jax
import jax.numpy as jnp
from jax import lax
from jax.experimental import pallas as pl
from jax.sharding import PartitionSpec as P

dilation_steps = (8, 16)


def padded_2(block, sides, width):
    for axis, dim in sides:
        count = lax.axis_size(axis)
        forward = [(i, i + 1) for i in range(count - 1)]
        backward = [(target, source) for source, target in forward]
        low = lax.ppermute(
            lax.slice_in_dim(block, block.shape[dim] - width, None, axis=dim), axis, forward
        )
        high = lax.ppermute(lax.slice_in_dim(block, 0, width, axis=dim), axis, backward)
        block = jnp.concatenate([low, block, high], axis=dim)
    return block


def gelu_value(values):
    return jax.nn.gelu(values, approximate=True)


def gelu_back(pre_values, upstream_gradient):
    return jax.vjp(gelu_value, pre_values)[1](upstream_gradient)[0]


def conv_forward_kernel(dilation, out_rows, act_ref, w_ref, scale_ref, shift_ref, out_ref):
    width = out_ref.shape[1]
    hidden = jnp.dot(act_ref[0:out_rows, :], w_ref[:, 0:width], preferred_element_type=jnp.float32)
    for kernel_tap in (1, 2):
        lower = kernel_tap * dilation
        hidden = hidden + jnp.dot(
            act_ref[lower : lower + out_rows, :],
            w_ref[:, kernel_tap * width : (kernel_tap + 1) * width],
            preferred_element_type=jnp.float32,
        )
    out_ref[...] = hidden * scale_ref[...] + shift_ref[...]


def conv_backward_kernel(dilation, out_rows, grad_ref, w_ref, out_ref):
    width = grad_ref.shape[1]
    numbers = (((1,), (1,)), ((), ()))
    total = None
    for kernel_tap in range(3):
        lower = (2 - kernel_tap) * dilation
        term = lax.dot_general(
            grad_ref[lower : lower + out_rows, :],
            w_ref[:, kernel_tap * width : (kernel_tap + 1) * width],
            numbers,
            preferred_element_type=jnp.float32,
        )
        total = term if total is None else total + term
    out_ref[...] = total


def conv_forward(padded, gathered, block, c2, scale, shift, dilation, out_rows):
    rows = gathered.shape[0]
    return pl.pallas_call(
        lambda *refs: conv_forward_kernel(dilation, out_rows, *refs),
        grid=(1,),
        in_specs=[
            pl.BlockSpec(padded.shape, lambda i: (0, 0)),
            pl.BlockSpec((rows, 3 * c2), lambda i: (0, block)),
            pl.BlockSpec((1, c2), lambda i: (0, 0)),
            pl.BlockSpec((1, c2), lambda i: (0, 0)),
        ],
        out_specs=pl.BlockSpec((out_rows, c2), lambda i: (0, 0)),
        out_shape=jax.ShapeDtypeStruct((out_rows, c2), jnp.float32),
    )(padded, gathered, scale.reshape(1, c2), shift.reshape(1, c2))


def conv_backward(d_pad, gathered, block, c2, dilation, out_rows):
    rows = gathered.shape[0]
    return pl.pallas_call(
        lambda *refs: conv_backward_kernel(dilation, out_rows, *refs),
        grid=(1,),
        in_specs=[
            pl.BlockSpec(d_pad.shape, lambda i: (0, 0)),
            pl.BlockSpec((rows, 3 * c2), lambda i: (0, block)),
        ],
        out_specs=pl.BlockSpec((out_rows, rows), lambda i: (0, 0)),
        out_shape=jax.ShapeDtypeStruct((out_rows, rows), jnp.float32),
    )(d_pad, gathered)


def mix_forward_kernel(dilation, middle_ref, w_ref, stream_ref, out_ref):
    rows = out_ref.shape[0]
    mixed = lax.dot_general(
        middle_ref[...], w_ref[...], (((1,), (1,)), ((), ())), preferred_element_type=jnp.float32
    )
    out_ref[...] = stream_ref[dilation : dilation + rows, :] + mixed


def mix_forward(middle, gathered, column_block, stream, dilation):
    rows, c2 = middle.shape
    channels = gathered.shape[0]
    return pl.pallas_call(
        lambda *refs: mix_forward_kernel(dilation, *refs),
        grid=(1,),
        in_specs=[
            pl.BlockSpec(middle.shape, lambda i: (0, 0)),
            pl.BlockSpec((channels, c2), lambda i: (0, column_block)),
            pl.BlockSpec(stream.shape, lambda i: (0, 0)),
        ],
        out_specs=pl.BlockSpec((rows, channels), lambda i: (0, 0)),
        out_shape=jax.ShapeDtypeStruct((rows, channels), jnp.float32),
    )(middle, gathered, stream)


def mix_backward_kernel(cot_ref, w_ref, out_ref):
    out_ref[...] = jnp.dot(cot_ref[...], w_ref[...], preferred_element_type=jnp.float32)


def mix_backward(cot_here, gathered, column_block, c2):
    rows = cot_here.shape[0]
    channels = gathered.shape[0]
    return pl.pallas_call(
        mix_backward_kernel,
        grid=(1,),
        in_specs=[
            pl.BlockSpec(cot_here.shape, lambda i: (0, 0)),
            pl.BlockSpec((channels, c2), lambda i: (0, column_block)),
        ],
        out_specs=pl.BlockSpec((rows, c2), lambda i: (0, 0)),
        out_shape=jax.ShapeDtypeStruct((rows, c2), jnp.float32),
    )(cot_here, gathered)


def fetch_weights(w_dilated, w_mix):
    blocks, rows, taps, c2 = w_dilated.shape
    local = jnp.concatenate(
        [w_dilated.reshape(blocks, rows, taps * c2).transpose(1, 0, 2).reshape(rows, -1),
         w_mix.transpose(1, 0, 2).reshape(rows, -1)],
        axis=1,
    )
    gathered = lax.all_gather(local, ("seq", "win"), axis=0, tiled=True)
    split = blocks * taps * c2
    return gathered, [gathered[:, split + b * c2 : split + (b + 1) * c2] for b in range(blocks)]


def shifted_taps(d_hidden, dilation):
    return jnp.concatenate(
        [jnp.pad(d_hidden, ((k * dilation, (2 - k) * dilation), (0, 0))) for k in range(3)], axis=1
    )


def gradient_kernel(scale, widths, *refs):
    out_ref = refs[-1]
    start = 0
    for pair in range(len(widths)):
        lhs = refs[2 * pair][...]
        rhs = refs[2 * pair + 1][...]
        term = jnp.dot(lhs, rhs, preferred_element_type=jnp.float32) * scale
        out_ref[:, start : start + widths[pair]] = term.astype(out_ref.dtype)
        start += widths[pair]


def weight_gradient_buffer(pairs, inverse_square_root, row_tile=256):
    rows = pairs[0][0].shape[0]
    widths = tuple(rhs.shape[1] for _, rhs in pairs)
    in_specs = []
    operands = []
    for lhs, rhs in pairs:
        in_specs.append(pl.BlockSpec((row_tile, lhs.shape[1]), lambda i: (i, 0)))
        in_specs.append(pl.BlockSpec(rhs.shape, lambda i: (0, 0)))
        operands += [lhs, rhs]
    return pl.pallas_call(
        lambda *refs: gradient_kernel(inverse_square_root, widths, *refs),
        grid=(rows // row_tile,),
        in_specs=in_specs,
        out_specs=pl.BlockSpec((row_tile, sum(widths)), lambda i: (i, 0)),
        out_shape=jax.ShapeDtypeStruct((rows, sum(widths)), jnp.bfloat16),
    )(*operands)


def per_device(inputs, cotangent, w_dilated, w_mix, in_scale, in_shift, mid_scale, mid_shift):
    x_local = inputs[0]
    cot_local = cotangent[0]
    row_count = x_local.shape[0]
    window_len = lax.axis_size("seq") * row_count
    inverse_square_root = 1.0 / math.sqrt(lax.axis_size("win") * inputs.shape[0] * window_len)
    residual_block_count = len(dilation_steps)
    saved = []
    gathered, mixing_weights = fetch_weights(w_dilated, w_mix)
    c2 = w_dilated.shape[3]
    mix_column = residual_block_count * w_dilated.shape[2]
    remaining = sum(dilation_steps)
    first_row = lax.axis_index("seq") * row_count
    stream = padded_2(x_local, (("seq", 0),), remaining).astype(jnp.float32)
    for residual_block_index in range(residual_block_count):
        dilation = dilation_steps[residual_block_index]
        w_out = mixing_weights[residual_block_index]
        pre_in = stream * in_scale[residual_block_index] + in_shift[residual_block_index]
        position = first_row - remaining + lax.broadcasted_iota(jnp.int32, (pre_in.shape[0], 1), 0)
        inside = (position >= 0) & (position < window_len)
        activated = jnp.where(inside, gelu_value(pre_in), 0.0).astype(jnp.bfloat16)
        out_rows = row_count + 2 * (remaining - dilation)
        pre_mid = conv_forward(
            activated,
            gathered,
            residual_block_index,
            c2,
            mid_scale[residual_block_index],
            mid_shift[residual_block_index],
            dilation,
            out_rows,
        )
        middle = gelu_value(pre_mid).astype(jnp.bfloat16)
        stream = mix_forward(middle, gathered, mix_column + residual_block_index, stream, dilation)
        own = remaining - dilation
        saved.append(
            (
                w_out,
                pre_in[remaining : remaining + row_count],
                activated[own : own + row_count + 2 * dilation],
                pre_mid[own : own + row_count],
                middle[own : own + row_count],
            )
        )
        remaining -= dilation
    output = stream.astype(jnp.bfloat16)
    upstream_gradient = cot_local.astype(jnp.float32)
    dilated_weight_gradients = [None] * residual_block_count
    mixing_weight_gradients = [None] * residual_block_count
    for residual_block_index in reversed(range(residual_block_count)):
        dilation = dilation_steps[residual_block_index]
        w_out, pre_in, padded, pre_mid, middle = saved[residual_block_index]
        cot_here = upstream_gradient.astype(jnp.bfloat16)
        d_mid = mix_backward(cot_here, gathered, mix_column + residual_block_index, c2)
        d_hidden = (gelu_back(pre_mid, d_mid) * mid_scale[residual_block_index]).astype(
            jnp.bfloat16
        )
        d_pad = padded_2(d_hidden, (("seq", 0),), dilation)
        d_act = conv_backward(d_pad, gathered, residual_block_index, c2, dilation, row_count)
        dilated_weight_gradients[residual_block_index] = (padded.T, shifted_taps(d_hidden, dilation))
        mixing_weight_gradients[residual_block_index] = (cot_here.T, middle)
        upstream_gradient = (
            upstream_gradient + gelu_back(pre_in, d_act) * in_scale[residual_block_index]
        )
    summed = lax.psum_scatter(
        weight_gradient_buffer(dilated_weight_gradients + mixing_weight_gradients, inverse_square_root),
        ("seq", "win"),
        scatter_dimension=0,
        tiled=True,
    ).astype(jnp.float32)
    own_rows = summed.shape[0]
    taps, c2 = w_dilated.shape[2], w_dilated.shape[3]
    split = residual_block_count * taps * c2
    return (
        output[None],
        upstream_gradient[None],
        summed[:, :split].reshape(own_rows, residual_block_count, taps, c2).transpose(1, 0, 2, 3),
        summed[:, split:].reshape(own_rows, residual_block_count, c2).transpose(1, 0, 2),
    )


def solution(mesh):
    in_specs = (
        P("win", "seq", None),
        P("win", "seq", None),
        P(None, ("seq", "win"), None, None),
        P(None, ("seq", "win"), None),
        P(),
        P(),
        P(),
        P(),
    )
    out_specs = (
        P("win", "seq", None),
        P("win", "seq", None),
        P(None, ("seq", "win"), None, None),
        P(None, ("seq", "win"), None),
    )
    return jax.shard_map(
        per_device, mesh=mesh, in_specs=in_specs, out_specs=out_specs, check_vma=False
    )
```

```python
import math

import jax
import jax.numpy as jnp
from jax import lax
from jax.experimental import pallas as pl
from jax.sharding import PartitionSpec as P

dilation_steps = (8, 16)


def padded_2(block, sides, width):
    for axis, dim in sides:
        count = lax.axis_size(axis)
        forward = [(i, i + 1) for i in range(count - 1)]
        backward = [(target, source) for source, target in forward]
        low = lax.ppermute(
            lax.slice_in_dim(block, block.shape[dim] - width, None, axis=dim), axis, forward
        )
        high = lax.ppermute(lax.slice_in_dim(block, 0, width, axis=dim), axis, backward)
        block = jnp.concatenate([low, block, high], axis=dim)
    return block


def gelu_value(values):
    return jax.nn.gelu(values, approximate=True)


def gelu_back(pre_values, upstream_gradient):
    return jax.vjp(gelu_value, pre_values)[1](upstream_gradient)[0]


def conv_forward_kernel(dilation, out_rows, act_ref, w_ref, scale_ref, shift_ref, out_ref):
    tap = pl.program_id(0)
    for kernel_tap in range(3):

        @pl.when(tap == kernel_tap)
        def _():
            lower = kernel_tap * dilation
            term = jnp.dot(
                act_ref[lower : lower + out_rows, :], w_ref[...], preferred_element_type=jnp.float32
            )
            if kernel_tap == 0:
                out_ref[...] = term
            elif kernel_tap == 1:
                out_ref[...] = out_ref[...] + term
            else:
                out_ref[...] = (out_ref[...] + term) * scale_ref[...] + shift_ref[...]


def conv_backward_kernel(dilation, out_rows, grad_ref, w_ref, out_ref):
    tap = pl.program_id(0)
    numbers = (((1,), (1,)), ((), ()))
    for kernel_tap in range(3):

        @pl.when(tap == kernel_tap)
        def _():
            lower = (2 - kernel_tap) * dilation
            term = lax.dot_general(
                grad_ref[lower : lower + out_rows, :],
                w_ref[...],
                numbers,
                preferred_element_type=jnp.float32,
            )
            if kernel_tap == 0:
                out_ref[...] = term
            else:
                out_ref[...] = out_ref[...] + term


def conv_forward(padded, gathered, block, c2, scale, shift, dilation, out_rows):
    rows = gathered.shape[0]
    return pl.pallas_call(
        lambda *refs: conv_forward_kernel(dilation, out_rows, *refs),
        grid=(3,),
        in_specs=[
            pl.BlockSpec(padded.shape, lambda k: (0, 0)),
            pl.BlockSpec((rows, c2), lambda k: (0, 3 * block + k)),
            pl.BlockSpec((1, c2), lambda k: (0, 0)),
            pl.BlockSpec((1, c2), lambda k: (0, 0)),
        ],
        out_specs=pl.BlockSpec((out_rows, c2), lambda k: (0, 0)),
        out_shape=jax.ShapeDtypeStruct((out_rows, c2), jnp.float32),
    )(padded, gathered, scale.reshape(1, c2), shift.reshape(1, c2))


def conv_backward(d_pad, gathered, block, c2, dilation, out_rows):
    rows = gathered.shape[0]
    return pl.pallas_call(
        lambda *refs: conv_backward_kernel(dilation, out_rows, *refs),
        grid=(3,),
        in_specs=[
            pl.BlockSpec(d_pad.shape, lambda k: (0, 0)),
            pl.BlockSpec((rows, c2), lambda k: (0, 3 * block + k)),
        ],
        out_specs=pl.BlockSpec((out_rows, rows), lambda k: (0, 0)),
        out_shape=jax.ShapeDtypeStruct((out_rows, rows), jnp.float32),
    )(d_pad, gathered)


def fetch_weights(w_dilated, w_mix):
    blocks, rows, taps, c2 = w_dilated.shape
    local = jnp.concatenate(
        [w_dilated.reshape(blocks, rows, taps * c2).transpose(1, 0, 2).reshape(rows, -1),
         w_mix.transpose(1, 0, 2).reshape(rows, -1)],
        axis=1,
    )
    gathered = lax.all_gather(local, ("seq", "win"), axis=0, tiled=True)
    split = blocks * taps * c2
    return gathered, [gathered[:, split + b * c2 : split + (b + 1) * c2] for b in range(blocks)]


def shifted_taps(d_hidden, dilation):
    return jnp.concatenate(
        [jnp.pad(d_hidden, ((k * dilation, (2 - k) * dilation), (0, 0))) for k in range(3)], axis=1
    )


def gradient_kernel(scale, widths, *refs):
    out_ref = refs[-1]
    start = 0
    for pair in range(len(widths)):
        lhs = refs[2 * pair][...]
        rhs = refs[2 * pair + 1][...]
        term = jnp.dot(lhs, rhs, preferred_element_type=jnp.float32) * scale
        out_ref[:, start : start + widths[pair]] = term.astype(out_ref.dtype)
        start += widths[pair]


def weight_gradient_buffer(pairs, inverse_square_root, row_tile=256):
    rows = pairs[0][0].shape[0]
    widths = tuple(rhs.shape[1] for _, rhs in pairs)
    in_specs = []
    operands = []
    for lhs, rhs in pairs:
        in_specs.append(pl.BlockSpec((row_tile, lhs.shape[1]), lambda i: (i, 0)))
        in_specs.append(pl.BlockSpec(rhs.shape, lambda i: (0, 0)))
        operands += [lhs, rhs]
    return pl.pallas_call(
        lambda *refs: gradient_kernel(inverse_square_root, widths, *refs),
        grid=(rows // row_tile,),
        in_specs=in_specs,
        out_specs=pl.BlockSpec((row_tile, sum(widths)), lambda i: (i, 0)),
        out_shape=jax.ShapeDtypeStruct((rows, sum(widths)), jnp.bfloat16),
    )(*operands)


def per_device(inputs, cotangent, w_dilated, w_mix, in_scale, in_shift, mid_scale, mid_shift):
    x_local = inputs[0]
    cot_local = cotangent[0]
    row_count = x_local.shape[0]
    window_len = lax.axis_size("seq") * row_count
    inverse_square_root = 1.0 / math.sqrt(lax.axis_size("win") * inputs.shape[0] * window_len)
    residual_block_count = len(dilation_steps)
    saved = []
    gathered, mixing_weights = fetch_weights(w_dilated, w_mix)
    c2 = w_dilated.shape[3]
    remaining = sum(dilation_steps)
    first_row = lax.axis_index("seq") * row_count
    stream = padded_2(x_local, (("seq", 0),), remaining).astype(jnp.float32)
    for residual_block_index in range(residual_block_count):
        dilation = dilation_steps[residual_block_index]
        w_out = mixing_weights[residual_block_index]
        pre_in = stream * in_scale[residual_block_index] + in_shift[residual_block_index]
        position = first_row - remaining + lax.broadcasted_iota(jnp.int32, (pre_in.shape[0], 1), 0)
        inside = (position >= 0) & (position < window_len)
        activated = jnp.where(inside, gelu_value(pre_in), 0.0).astype(jnp.bfloat16)
        out_rows = row_count + 2 * (remaining - dilation)
        pre_mid = conv_forward(
            activated,
            gathered,
            residual_block_index,
            c2,
            mid_scale[residual_block_index],
            mid_shift[residual_block_index],
            dilation,
            out_rows,
        )
        middle = gelu_value(pre_mid).astype(jnp.bfloat16)
        stream = stream[dilation : dilation + out_rows] + jnp.einsum(
            "pe,ce->pc", middle, w_out, preferred_element_type=jnp.float32
        )
        own = remaining - dilation
        saved.append(
            (
                w_out,
                pre_in[remaining : remaining + row_count],
                activated[own : own + row_count + 2 * dilation],
                pre_mid[own : own + row_count],
                middle[own : own + row_count],
            )
        )
        remaining -= dilation
    output = stream.astype(jnp.bfloat16)
    upstream_gradient = cot_local.astype(jnp.float32)
    dilated_weight_gradients = [None] * residual_block_count
    mixing_weight_gradients = [None] * residual_block_count
    for residual_block_index in reversed(range(residual_block_count)):
        dilation = dilation_steps[residual_block_index]
        w_out, pre_in, padded, pre_mid, middle = saved[residual_block_index]
        cot_here = upstream_gradient.astype(jnp.bfloat16)
        d_mid = jnp.dot(cot_here, w_out, preferred_element_type=jnp.float32)
        d_hidden = (gelu_back(pre_mid, d_mid) * mid_scale[residual_block_index]).astype(
            jnp.bfloat16
        )
        d_pad = padded_2(d_hidden, (("seq", 0),), dilation)
        d_act = conv_backward(d_pad, gathered, residual_block_index, c2, dilation, row_count)
        dilated_weight_gradients[residual_block_index] = (padded.T, shifted_taps(d_hidden, dilation))
        mixing_weight_gradients[residual_block_index] = (cot_here.T, middle)
        upstream_gradient = (
            upstream_gradient + gelu_back(pre_in, d_act) * in_scale[residual_block_index]
        )
    summed = lax.psum_scatter(
        weight_gradient_buffer(dilated_weight_gradients + mixing_weight_gradients, inverse_square_root),
        ("seq", "win"),
        scatter_dimension=0,
        tiled=True,
    ).astype(jnp.float32)
    own_rows = summed.shape[0]
    taps, c2 = w_dilated.shape[2], w_dilated.shape[3]
    split = residual_block_count * taps * c2
    return (
        output[None],
        upstream_gradient[None],
        summed[:, :split].reshape(own_rows, residual_block_count, taps, c2).transpose(1, 0, 2, 3),
        summed[:, split:].reshape(own_rows, residual_block_count, c2).transpose(1, 0, 2),
    )


def solution(mesh):
    in_specs = (
        P("win", "seq", None),
        P("win", "seq", None),
        P(None, ("seq", "win"), None, None),
        P(None, ("seq", "win"), None),
        P(),
        P(),
        P(),
        P(),
    )
    out_specs = (
        P("win", "seq", None),
        P("win", "seq", None),
        P(None, ("seq", "win"), None, None),
        P(None, ("seq", "win"), None),
    )
    return jax.shard_map(
        per_device, mesh=mesh, in_specs=in_specs, out_specs=out_specs, check_vma=False
    )
```

```python
import math

import jax
import jax.numpy as jnp
from jax import lax
from jax.experimental import pallas as pl
from jax.sharding import PartitionSpec as P

dilation_steps = (8, 16)


def padded_2(block, sides, width):
    for axis, dim in sides:
        count = lax.axis_size(axis)
        forward = [(i, i + 1) for i in range(count - 1)]
        backward = [(target, source) for source, target in forward]
        low = lax.ppermute(
            lax.slice_in_dim(block, block.shape[dim] - width, None, axis=dim), axis, forward
        )
        high = lax.ppermute(lax.slice_in_dim(block, 0, width, axis=dim), axis, backward)
        block = jnp.concatenate([low, block, high], axis=dim)
    return block


def gelu_value(values):
    return jax.nn.gelu(values, approximate=True)


def gelu_back(pre_values, upstream_gradient):
    return jax.vjp(gelu_value, pre_values)[1](upstream_gradient)[0]


def conv_forward_kernel(dilation, out_rows, act_ref, w_ref, scale_ref, shift_ref, out_ref):
    tap = pl.program_id(0)
    for kernel_tap in range(3):

        @pl.when(tap == kernel_tap)
        def _():
            lower = kernel_tap * dilation
            term = jnp.dot(
                act_ref[lower : lower + out_rows, :], w_ref[...], preferred_element_type=jnp.float32
            )
            if kernel_tap == 0:
                out_ref[...] = term
            elif kernel_tap == 1:
                out_ref[...] = out_ref[...] + term
            else:
                out_ref[...] = (out_ref[...] + term) * scale_ref[...] + shift_ref[...]


def conv_backward_kernel(dilation, out_rows, grad_ref, w_ref, out_ref):
    tap = pl.program_id(0)
    numbers = (((1,), (1,)), ((), ()))
    for kernel_tap in range(3):

        @pl.when(tap == kernel_tap)
        def _():
            lower = (2 - kernel_tap) * dilation
            term = lax.dot_general(
                grad_ref[lower : lower + out_rows, :],
                w_ref[...],
                numbers,
                preferred_element_type=jnp.float32,
            )
            if kernel_tap == 0:
                out_ref[...] = term
            else:
                out_ref[...] = out_ref[...] + term


def conv_forward(padded, gathered, block, c2, scale, shift, dilation, out_rows):
    rows = gathered.shape[0]
    return pl.pallas_call(
        lambda *refs: conv_forward_kernel(dilation, out_rows, *refs),
        grid=(3,),
        in_specs=[
            pl.BlockSpec(padded.shape, lambda k: (0, 0)),
            pl.BlockSpec((rows, c2), lambda k: (0, 3 * block + k)),
            pl.BlockSpec((1, c2), lambda k: (0, 0)),
            pl.BlockSpec((1, c2), lambda k: (0, 0)),
        ],
        out_specs=pl.BlockSpec((out_rows, c2), lambda k: (0, 0)),
        out_shape=jax.ShapeDtypeStruct((out_rows, c2), jnp.float32),
    )(padded, gathered, scale.reshape(1, c2), shift.reshape(1, c2))


def conv_backward(d_pad, gathered, block, c2, dilation, out_rows):
    rows = gathered.shape[0]
    return pl.pallas_call(
        lambda *refs: conv_backward_kernel(dilation, out_rows, *refs),
        grid=(3,),
        in_specs=[
            pl.BlockSpec(d_pad.shape, lambda k: (0, 0)),
            pl.BlockSpec((rows, c2), lambda k: (0, 3 * block + k)),
        ],
        out_specs=pl.BlockSpec((out_rows, rows), lambda k: (0, 0)),
        out_shape=jax.ShapeDtypeStruct((out_rows, rows), jnp.float32),
    )(d_pad, gathered)


def fetch_weights(w_dilated, w_mix):
    blocks, rows, taps, c2 = w_dilated.shape
    local = jnp.concatenate(
        [w_dilated.reshape(blocks, rows, taps * c2).transpose(1, 0, 2).reshape(rows, -1),
         w_mix.transpose(1, 0, 2).reshape(rows, -1)],
        axis=1,
    )
    gathered = lax.all_gather(local, ("seq", "win"), axis=0, tiled=True)
    split = blocks * taps * c2
    return gathered, [gathered[:, split + b * c2 : split + (b + 1) * c2] for b in range(blocks)]


def shifted_taps(d_hidden, dilation):
    return jnp.concatenate(
        [jnp.pad(d_hidden, ((k * dilation, (2 - k) * dilation), (0, 0))) for k in range(3)], axis=1
    )


def gradient_kernel(scale, layout, count, *refs):
    out_refs = refs[2 * count :]
    for pair, (target, start, width) in enumerate(layout):
        lhs = refs[2 * pair][...]
        rhs = refs[2 * pair + 1][...]
        term = jnp.dot(lhs, rhs, preferred_element_type=jnp.float32) * scale
        out_refs[target][:, start : start + width] = term.astype(out_refs[target].dtype)


def weight_gradient_buffers(groups, inverse_square_root, row_tile=256):
    rows = groups[0][0][0].shape[0]
    layout = []
    in_specs = []
    operands = []
    widths = []
    for target, group in enumerate(groups):
        start = 0
        for lhs, rhs in group:
            layout.append((target, start, rhs.shape[1]))
            start += rhs.shape[1]
            in_specs.append(pl.BlockSpec((row_tile, lhs.shape[1]), lambda i: (i, 0)))
            in_specs.append(pl.BlockSpec(rhs.shape, lambda i: (0, 0)))
            operands += [lhs, rhs]
        widths.append(start)
    return pl.pallas_call(
        lambda *refs: gradient_kernel(inverse_square_root, tuple(layout), len(layout), *refs),
        grid=(rows // row_tile,),
        in_specs=in_specs,
        out_specs=[pl.BlockSpec((row_tile, w), lambda i: (i, 0)) for w in widths],
        out_shape=[jax.ShapeDtypeStruct((rows, w), jnp.bfloat16) for w in widths],
    )(*operands)


def scatter_by_exchange(buffer, axes):
    count = lax.axis_size(axes)
    pieces = buffer.reshape(count, buffer.shape[0] // count, buffer.shape[1])
    received = lax.all_to_all(pieces, axes, 0, 0, tiled=False)
    return jnp.sum(received.astype(jnp.float32), axis=0)


def per_device(inputs, cotangent, w_dilated, w_mix, in_scale, in_shift, mid_scale, mid_shift):
    x_local = inputs[0]
    cot_local = cotangent[0]
    row_count = x_local.shape[0]
    window_len = lax.axis_size("seq") * row_count
    inverse_square_root = 1.0 / math.sqrt(lax.axis_size("win") * inputs.shape[0] * window_len)
    residual_block_count = len(dilation_steps)
    saved = []
    gathered, mixing_weights = fetch_weights(w_dilated, w_mix)
    c2 = w_dilated.shape[3]
    remaining = sum(dilation_steps)
    first_row = lax.axis_index("seq") * row_count
    stream = padded_2(x_local, (("seq", 0),), remaining).astype(jnp.float32)
    for residual_block_index in range(residual_block_count):
        dilation = dilation_steps[residual_block_index]
        w_out = mixing_weights[residual_block_index]
        pre_in = stream * in_scale[residual_block_index] + in_shift[residual_block_index]
        position = first_row - remaining + lax.broadcasted_iota(jnp.int32, (pre_in.shape[0], 1), 0)
        inside = (position >= 0) & (position < window_len)
        activated = jnp.where(inside, gelu_value(pre_in), 0.0).astype(jnp.bfloat16)
        out_rows = row_count + 2 * (remaining - dilation)
        pre_mid = conv_forward(
            activated,
            gathered,
            residual_block_index,
            c2,
            mid_scale[residual_block_index],
            mid_shift[residual_block_index],
            dilation,
            out_rows,
        )
        middle = gelu_value(pre_mid).astype(jnp.bfloat16)
        stream = stream[dilation : dilation + out_rows] + jnp.einsum(
            "pe,ce->pc", middle, w_out, preferred_element_type=jnp.float32
        )
        own = remaining - dilation
        saved.append(
            (
                w_out,
                pre_in[remaining : remaining + row_count],
                activated[own : own + row_count + 2 * dilation],
                pre_mid[own : own + row_count],
                middle[own : own + row_count],
            )
        )
        remaining -= dilation
    output = stream.astype(jnp.bfloat16)
    upstream_gradient = cot_local.astype(jnp.float32)
    dilated_weight_gradients = [None] * residual_block_count
    mixing_weight_gradients = [None] * residual_block_count
    for residual_block_index in reversed(range(residual_block_count)):
        dilation = dilation_steps[residual_block_index]
        w_out, pre_in, padded, pre_mid, middle = saved[residual_block_index]
        cot_here = upstream_gradient.astype(jnp.bfloat16)
        d_mid = jnp.dot(cot_here, w_out, preferred_element_type=jnp.float32)
        d_hidden = (gelu_back(pre_mid, d_mid) * mid_scale[residual_block_index]).astype(
            jnp.bfloat16
        )
        d_pad = padded_2(d_hidden, (("seq", 0),), dilation)
        d_act = conv_backward(d_pad, gathered, residual_block_index, c2, dilation, row_count)
        dilated_weight_gradients[residual_block_index] = (padded.T, shifted_taps(d_hidden, dilation))
        mixing_weight_gradients[residual_block_index] = (cot_here.T, middle)
        upstream_gradient = (
            upstream_gradient + gelu_back(pre_in, d_act) * in_scale[residual_block_index]
        )
    first, second = weight_gradient_buffers(
        [
            [dilated_weight_gradients[0]] + mixing_weight_gradients,
            dilated_weight_gradients[1:],
        ],
        inverse_square_root,
    )
    summed_first = lax.psum_scatter(
        first, ("seq", "win"), scatter_dimension=0, tiled=True
    ).astype(jnp.float32)
    summed_second = scatter_by_exchange(second, ("seq", "win"))
    own_rows = summed_first.shape[0]
    taps, c2 = w_dilated.shape[2], w_dilated.shape[3]
    width = taps * c2
    dilated = jnp.stack(
        [summed_first[:, :width], summed_second[:, :width]]
    ).reshape(residual_block_count, own_rows, taps, c2)
    mixing = summed_first[:, width:].reshape(own_rows, residual_block_count, c2).transpose(1, 0, 2)
    return (
        output[None],
        upstream_gradient[None],
        dilated,
        mixing,
    )


def solution(mesh):
    in_specs = (
        P("win", "seq", None),
        P("win", "seq", None),
        P(None, ("seq", "win"), None, None),
        P(None, ("seq", "win"), None),
        P(),
        P(),
        P(),
        P(),
    )
    out_specs = (
        P("win", "seq", None),
        P("win", "seq", None),
        P(None, ("seq", "win"), None, None),
        P(None, ("seq", "win"), None),
    )
    return jax.shard_map(
        per_device, mesh=mesh, in_specs=in_specs, out_specs=out_specs, check_vma=False
    )
```

```python
import math

import jax
import jax.numpy as jnp
from jax import lax
from jax.experimental import pallas as pl
from jax.sharding import PartitionSpec as P

dilation_steps = (8, 16)
WIN = ("y", "core")
ALL = ("seq", "y", "core")


def padded_2(block, sides, width):
    for axis, dim in sides:
        count = lax.axis_size(axis)
        forward = [(i, i + 1) for i in range(count - 1)]
        backward = [(target, source) for source, target in forward]
        low = lax.ppermute(
            lax.slice_in_dim(block, block.shape[dim] - width, None, axis=dim), axis, forward
        )
        high = lax.ppermute(lax.slice_in_dim(block, 0, width, axis=dim), axis, backward)
        block = jnp.concatenate([low, block, high], axis=dim)
    return block


def gelu_value(values):
    return jax.nn.gelu(values, approximate=True)


def gelu_back(pre_values, upstream_gradient):
    return jax.vjp(gelu_value, pre_values)[1](upstream_gradient)[0]


def conv_forward_kernel(dilation, out_rows, act_ref, w_ref, scale_ref, shift_ref, out_ref):
    tap = pl.program_id(0)
    for kernel_tap in range(3):

        @pl.when(tap == kernel_tap)
        def _():
            lower = kernel_tap * dilation
            term = jnp.dot(
                act_ref[lower : lower + out_rows, :], w_ref[...], preferred_element_type=jnp.float32
            )
            if kernel_tap == 0:
                out_ref[...] = term
            elif kernel_tap == 1:
                out_ref[...] = out_ref[...] + term
            else:
                out_ref[...] = (out_ref[...] + term) * scale_ref[...] + shift_ref[...]


def conv_backward_kernel(dilation, out_rows, grad_ref, w_ref, out_ref):
    tap = pl.program_id(0)
    numbers = (((1,), (1,)), ((), ()))
    for kernel_tap in range(3):

        @pl.when(tap == kernel_tap)
        def _():
            lower = (2 - kernel_tap) * dilation
            term = lax.dot_general(
                grad_ref[lower : lower + out_rows, :],
                w_ref[...],
                numbers,
                preferred_element_type=jnp.float32,
            )
            if kernel_tap == 0:
                out_ref[...] = term
            else:
                out_ref[...] = out_ref[...] + term


def conv_forward(padded, gathered, block, c2, scale, shift, dilation, out_rows):
    rows = gathered.shape[0]
    return pl.pallas_call(
        lambda *refs: conv_forward_kernel(dilation, out_rows, *refs),
        grid=(3,),
        in_specs=[
            pl.BlockSpec(padded.shape, lambda k: (0, 0)),
            pl.BlockSpec((rows, c2), lambda k: (0, 3 * block + k)),
            pl.BlockSpec((1, c2), lambda k: (0, 0)),
            pl.BlockSpec((1, c2), lambda k: (0, 0)),
        ],
        out_specs=pl.BlockSpec((out_rows, c2), lambda k: (0, 0)),
        out_shape=jax.ShapeDtypeStruct((out_rows, c2), jnp.float32),
    )(padded, gathered, scale.reshape(1, c2), shift.reshape(1, c2))


def conv_backward(d_pad, gathered, block, c2, dilation, out_rows):
    rows = gathered.shape[0]
    return pl.pallas_call(
        lambda *refs: conv_backward_kernel(dilation, out_rows, *refs),
        grid=(3,),
        in_specs=[
            pl.BlockSpec(d_pad.shape, lambda k: (0, 0)),
            pl.BlockSpec((rows, c2), lambda k: (0, 3 * block + k)),
        ],
        out_specs=pl.BlockSpec((out_rows, rows), lambda k: (0, 0)),
        out_shape=jax.ShapeDtypeStruct((out_rows, rows), jnp.float32),
    )(d_pad, gathered)


def fetch_weights(w_dilated, w_mix):
    blocks, rows, taps, c2 = w_dilated.shape
    local = jnp.concatenate(
        [w_dilated.reshape(blocks, rows, taps * c2).transpose(1, 0, 2).reshape(rows, -1),
         w_mix.transpose(1, 0, 2).reshape(rows, -1)],
        axis=1,
    )
    gathered = lax.all_gather(local, ALL, axis=0, tiled=True)
    split = blocks * taps * c2
    return gathered, [gathered[:, split + b * c2 : split + (b + 1) * c2] for b in range(blocks)]


def shifted_taps(d_hidden, dilation):
    return jnp.concatenate(
        [jnp.pad(d_hidden, ((k * dilation, (2 - k) * dilation), (0, 0))) for k in range(3)], axis=1
    )


def gradient_kernel(scale, widths, *refs):
    out_ref = refs[-1]
    start = 0
    for pair in range(len(widths)):
        lhs = refs[2 * pair][...]
        rhs = refs[2 * pair + 1][...]
        term = jnp.dot(lhs, rhs, preferred_element_type=jnp.float32) * scale
        out_ref[:, start : start + widths[pair]] = term.astype(out_ref.dtype)
        start += widths[pair]


def weight_gradient_buffer(pairs, inverse_square_root, row_tile=256):
    rows = pairs[0][0].shape[0]
    widths = tuple(rhs.shape[1] for _, rhs in pairs)
    in_specs = []
    operands = []
    for lhs, rhs in pairs:
        in_specs.append(pl.BlockSpec((row_tile, lhs.shape[1]), lambda i: (i, 0)))
        in_specs.append(pl.BlockSpec(rhs.shape, lambda i: (0, 0)))
        operands += [lhs, rhs]
    return pl.pallas_call(
        lambda *refs: gradient_kernel(inverse_square_root, widths, *refs),
        grid=(rows // row_tile,),
        in_specs=in_specs,
        out_specs=pl.BlockSpec((row_tile, sum(widths)), lambda i: (i, 0)),
        out_shape=jax.ShapeDtypeStruct((rows, sum(widths)), jnp.bfloat16),
    )(*operands)


def own_first(rows_by_channel):
    cores = lax.axis_size("core")
    core = lax.axis_index("core")
    grouped = rows_by_channel.reshape(-1, cores, rows_by_channel.shape[0] // (cores * lax.axis_size(("seq", "y"))), rows_by_channel.shape[1])
    order = (core + jnp.arange(cores)) % cores
    return jnp.take(grouped, order, axis=1).transpose(1, 0, 2, 3).reshape(rows_by_channel.shape)


def per_device(inputs, cotangent, w_dilated, w_mix, in_scale, in_shift, mid_scale, mid_shift):
    x_local = inputs[0]
    cot_local = cotangent[0]
    row_count = x_local.shape[0]
    window_len = lax.axis_size("seq") * row_count
    inverse_square_root = 1.0 / math.sqrt(lax.axis_size("y") * lax.axis_size("core") * inputs.shape[0] * window_len)
    residual_block_count = len(dilation_steps)
    saved = []
    gathered, mixing_weights = fetch_weights(w_dilated, w_mix)
    c2 = w_dilated.shape[3]
    remaining = sum(dilation_steps)
    first_row = lax.axis_index("seq") * row_count
    stream = padded_2(x_local, (("seq", 0),), remaining).astype(jnp.float32)
    for residual_block_index in range(residual_block_count):
        dilation = dilation_steps[residual_block_index]
        w_out = mixing_weights[residual_block_index]
        pre_in = stream * in_scale[residual_block_index] + in_shift[residual_block_index]
        position = first_row - remaining + lax.broadcasted_iota(jnp.int32, (pre_in.shape[0], 1), 0)
        inside = (position >= 0) & (position < window_len)
        activated = jnp.where(inside, gelu_value(pre_in), 0.0).astype(jnp.bfloat16)
        out_rows = row_count + 2 * (remaining - dilation)
        pre_mid = conv_forward(
            activated,
            gathered,
            residual_block_index,
            c2,
            mid_scale[residual_block_index],
            mid_shift[residual_block_index],
            dilation,
            out_rows,
        )
        middle = gelu_value(pre_mid).astype(jnp.bfloat16)
        stream = stream[dilation : dilation + out_rows] + jnp.einsum(
            "pe,ce->pc", middle, w_out, preferred_element_type=jnp.float32
        )
        own = remaining - dilation
        saved.append(
            (
                w_out,
                pre_in[remaining : remaining + row_count],
                activated[own : own + row_count + 2 * dilation],
                pre_mid[own : own + row_count],
                middle[own : own + row_count],
            )
        )
        remaining -= dilation
    output = stream.astype(jnp.bfloat16)
    upstream_gradient = cot_local.astype(jnp.float32)
    dilated_weight_gradients = [None] * residual_block_count
    mixing_weight_gradients = [None] * residual_block_count
    for residual_block_index in reversed(range(residual_block_count)):
        dilation = dilation_steps[residual_block_index]
        w_out, pre_in, padded, pre_mid, middle = saved[residual_block_index]
        cot_here = upstream_gradient.astype(jnp.bfloat16)
        d_mid = jnp.dot(cot_here, w_out, preferred_element_type=jnp.float32)
        d_hidden = (gelu_back(pre_mid, d_mid) * mid_scale[residual_block_index]).astype(
            jnp.bfloat16
        )
        d_pad = padded_2(d_hidden, (("seq", 0),), dilation)
        d_act = conv_backward(d_pad, gathered, residual_block_index, c2, dilation, row_count)
        dilated_weight_gradients[residual_block_index] = (own_first(padded.T), shifted_taps(d_hidden, dilation))
        mixing_weight_gradients[residual_block_index] = (own_first(cot_here.T), middle)
        upstream_gradient = (
            upstream_gradient + gelu_back(pre_in, d_act) * in_scale[residual_block_index]
        )
    buffer = weight_gradient_buffer(dilated_weight_gradients + mixing_weight_gradients, inverse_square_root)
    half = buffer.shape[0] // lax.axis_size("core")
    partner = lax.ppermute(buffer[half:], "core", [(0, 1), (1, 0)])
    paired = (buffer[:half].astype(jnp.float32) + partner.astype(jnp.float32)).astype(jnp.bfloat16)
    summed = lax.psum_scatter(paired, ("seq", "y"), scatter_dimension=0, tiled=True).astype(jnp.float32)
    own_rows = summed.shape[0]
    taps, c2 = w_dilated.shape[2], w_dilated.shape[3]
    split = residual_block_count * taps * c2
    return (
        output[None],
        upstream_gradient[None],
        summed[:, :split].reshape(own_rows, residual_block_count, taps, c2).transpose(1, 0, 2, 3),
        summed[:, split:].reshape(own_rows, residual_block_count, c2).transpose(1, 0, 2),
    )


def solution(mesh):
    win = mesh.shape["win"]
    grid = jax.sharding.Mesh(mesh.devices.reshape(mesh.shape["seq"], win // 2, 2), ALL)
    in_specs = (
        P(WIN, "seq", None),
        P(WIN, "seq", None),
        P(None, ALL, None, None),
        P(None, ALL, None),
        P(),
        P(),
        P(),
        P(),
    )
    out_specs = (
        P(WIN, "seq", None),
        P(WIN, "seq", None),
        P(None, ALL, None, None),
        P(None, ALL, None),
    )
    return jax.shard_map(
        per_device, mesh=grid, in_specs=in_specs, out_specs=out_specs, check_vma=False
    )
```

```python
import math

import jax
import jax.numpy as jnp
from jax import lax
from jax.experimental import pallas as pl
from jax.sharding import PartitionSpec as P

dilation_steps = (8, 16)
WIN = ("y", "core")
ALL = ("seq", "y", "core")


def padded_2(block, sides, width):
    for axis, dim in sides:
        count = lax.axis_size(axis)
        forward = [(i, i + 1) for i in range(count - 1)]
        backward = [(target, source) for source, target in forward]
        low = lax.ppermute(
            lax.slice_in_dim(block, block.shape[dim] - width, None, axis=dim), axis, forward
        )
        high = lax.ppermute(lax.slice_in_dim(block, 0, width, axis=dim), axis, backward)
        block = jnp.concatenate([low, block, high], axis=dim)
    return block


def gelu_value(values):
    return jax.nn.gelu(values, approximate=True)


def gelu_back(pre_values, upstream_gradient):
    return jax.vjp(gelu_value, pre_values)[1](upstream_gradient)[0]


def conv_forward_kernel(dilation, out_rows, act_ref, w_ref, scale_ref, shift_ref, out_ref):
    tap = pl.program_id(0)
    for kernel_tap in range(3):

        @pl.when(tap == kernel_tap)
        def _():
            lower = kernel_tap * dilation
            term = jnp.dot(
                act_ref[lower : lower + out_rows, :], w_ref[...], preferred_element_type=jnp.float32
            )
            if kernel_tap == 0:
                out_ref[...] = term
            elif kernel_tap == 1:
                out_ref[...] = out_ref[...] + term
            else:
                out_ref[...] = (out_ref[...] + term) * scale_ref[...] + shift_ref[...]


def conv_backward_kernel(dilation, out_rows, grad_ref, w_ref, out_ref):
    tap = pl.program_id(0)
    numbers = (((1,), (1,)), ((), ()))
    for kernel_tap in range(3):

        @pl.when(tap == kernel_tap)
        def _():
            lower = (2 - kernel_tap) * dilation
            term = lax.dot_general(
                grad_ref[lower : lower + out_rows, :],
                w_ref[...],
                numbers,
                preferred_element_type=jnp.float32,
            )
            if kernel_tap == 0:
                out_ref[...] = term
            else:
                out_ref[...] = out_ref[...] + term


def conv_forward(padded, gathered, block, c2, scale, shift, dilation, out_rows):
    rows = gathered.shape[0]
    return pl.pallas_call(
        lambda *refs: conv_forward_kernel(dilation, out_rows, *refs),
        grid=(3,),
        in_specs=[
            pl.BlockSpec(padded.shape, lambda k: (0, 0)),
            pl.BlockSpec((rows, c2), lambda k: (0, 3 * block + k)),
            pl.BlockSpec((1, c2), lambda k: (0, 0)),
            pl.BlockSpec((1, c2), lambda k: (0, 0)),
        ],
        out_specs=pl.BlockSpec((out_rows, c2), lambda k: (0, 0)),
        out_shape=jax.ShapeDtypeStruct((out_rows, c2), jnp.float32),
    )(padded, gathered, scale.reshape(1, c2), shift.reshape(1, c2))


def conv_backward(d_pad, gathered, block, c2, dilation, out_rows):
    rows = gathered.shape[0]
    return pl.pallas_call(
        lambda *refs: conv_backward_kernel(dilation, out_rows, *refs),
        grid=(3,),
        in_specs=[
            pl.BlockSpec(d_pad.shape, lambda k: (0, 0)),
            pl.BlockSpec((rows, c2), lambda k: (0, 3 * block + k)),
        ],
        out_specs=pl.BlockSpec((out_rows, rows), lambda k: (0, 0)),
        out_shape=jax.ShapeDtypeStruct((out_rows, rows), jnp.float32),
    )(d_pad, gathered)


def fetch_weights(w_dilated, w_mix):
    blocks, rows, taps, c2 = w_dilated.shape
    local = jnp.concatenate(
        [w_dilated.reshape(blocks, rows, taps * c2).transpose(1, 0, 2).reshape(rows, -1),
         w_mix.transpose(1, 0, 2).reshape(rows, -1)],
        axis=1,
    )
    gathered = lax.all_gather(local, ALL, axis=0, tiled=True)
    split = blocks * taps * c2
    return gathered, [gathered[:, split + b * c2 : split + (b + 1) * c2] for b in range(blocks)]


def shifted_taps(d_hidden, dilation):
    return jnp.concatenate(
        [jnp.pad(d_hidden, ((k * dilation, (2 - k) * dilation), (0, 0))) for k in range(3)], axis=1
    )


def gradient_kernel(scale, widths, *refs):
    out_ref = refs[-1]
    start = 0
    for pair in range(len(widths)):
        lhs = refs[2 * pair][...]
        rhs = refs[2 * pair + 1][...]
        term = jnp.dot(lhs, rhs, preferred_element_type=jnp.float32) * scale
        out_ref[:, start : start + widths[pair]] = term.astype(out_ref.dtype)
        start += widths[pair]


def weight_gradient_buffer(pairs, inverse_square_root, first_tile, tiles, row_tile=256):
    widths = tuple(rhs.shape[1] for _, rhs in pairs)
    in_specs = []
    operands = []
    for lhs, rhs in pairs:
        in_specs.append(pl.BlockSpec((row_tile, lhs.shape[1]), lambda i: (i + first_tile, 0)))
        in_specs.append(pl.BlockSpec(rhs.shape, lambda i: (0, 0)))
        operands += [lhs, rhs]
    return pl.pallas_call(
        lambda *refs: gradient_kernel(inverse_square_root, widths, *refs),
        grid=(tiles,),
        in_specs=in_specs,
        out_specs=pl.BlockSpec((row_tile, sum(widths)), lambda i: (i, 0)),
        out_shape=jax.ShapeDtypeStruct((tiles * row_tile, sum(widths)), jnp.bfloat16),
    )(*operands)


def own_first(rows_by_channel):
    cores = lax.axis_size("core")
    core = lax.axis_index("core")
    grouped = rows_by_channel.reshape(-1, cores, rows_by_channel.shape[0] // (cores * lax.axis_size(("seq", "y"))), rows_by_channel.shape[1])
    order = (core + jnp.arange(cores)) % cores
    return jnp.take(grouped, order, axis=1).transpose(1, 0, 2, 3).reshape(rows_by_channel.shape)


def per_device(inputs, cotangent, w_dilated, w_mix, in_scale, in_shift, mid_scale, mid_shift):
    x_local = inputs[0]
    cot_local = cotangent[0]
    row_count = x_local.shape[0]
    window_len = lax.axis_size("seq") * row_count
    inverse_square_root = 1.0 / math.sqrt(lax.axis_size("y") * lax.axis_size("core") * inputs.shape[0] * window_len)
    residual_block_count = len(dilation_steps)
    saved = []
    gathered, mixing_weights = fetch_weights(w_dilated, w_mix)
    c2 = w_dilated.shape[3]
    remaining = sum(dilation_steps)
    first_row = lax.axis_index("seq") * row_count
    stream = padded_2(x_local, (("seq", 0),), remaining).astype(jnp.float32)
    for residual_block_index in range(residual_block_count):
        dilation = dilation_steps[residual_block_index]
        w_out = mixing_weights[residual_block_index]
        pre_in = stream * in_scale[residual_block_index] + in_shift[residual_block_index]
        position = first_row - remaining + lax.broadcasted_iota(jnp.int32, (pre_in.shape[0], 1), 0)
        inside = (position >= 0) & (position < window_len)
        activated = jnp.where(inside, gelu_value(pre_in), 0.0).astype(jnp.bfloat16)
        out_rows = row_count + 2 * (remaining - dilation)
        pre_mid = conv_forward(
            activated,
            gathered,
            residual_block_index,
            c2,
            mid_scale[residual_block_index],
            mid_shift[residual_block_index],
            dilation,
            out_rows,
        )
        middle = gelu_value(pre_mid).astype(jnp.bfloat16)
        stream = stream[dilation : dilation + out_rows] + jnp.einsum(
            "pe,ce->pc", middle, w_out, preferred_element_type=jnp.float32
        )
        own = remaining - dilation
        saved.append(
            (
                w_out,
                pre_in[remaining : remaining + row_count],
                activated[own : own + row_count + 2 * dilation],
                pre_mid[own : own + row_count],
                middle[own : own + row_count],
            )
        )
        remaining -= dilation
    output = stream.astype(jnp.bfloat16)
    upstream_gradient = cot_local.astype(jnp.float32)
    dilated_weight_gradients = [None] * residual_block_count
    mixing_weight_gradients = [None] * residual_block_count
    for residual_block_index in reversed(range(residual_block_count)):
        dilation = dilation_steps[residual_block_index]
        w_out, pre_in, padded, pre_mid, middle = saved[residual_block_index]
        cot_here = upstream_gradient.astype(jnp.bfloat16)
        d_mid = jnp.dot(cot_here, w_out, preferred_element_type=jnp.float32)
        d_hidden = (gelu_back(pre_mid, d_mid) * mid_scale[residual_block_index]).astype(
            jnp.bfloat16
        )
        d_pad = padded_2(d_hidden, (("seq", 0),), dilation)
        d_act = conv_backward(d_pad, gathered, residual_block_index, c2, dilation, row_count)
        dilated_weight_gradients[residual_block_index] = (own_first(padded.T), shifted_taps(d_hidden, dilation))
        mixing_weight_gradients[residual_block_index] = (own_first(cot_here.T), middle)
        upstream_gradient = (
            upstream_gradient + gelu_back(pre_in, d_act) * in_scale[residual_block_index]
        )
    pairs = dilated_weight_gradients + mixing_weight_gradients
    row_tile = 256
    tiles = pairs[0][0].shape[0] // (row_tile * lax.axis_size("core"))
    partner_rows = weight_gradient_buffer(pairs, inverse_square_root, tiles, tiles, row_tile)
    partner = lax.ppermute(partner_rows, "core", [(0, 1), (1, 0)])
    own_rows = weight_gradient_buffer(pairs, inverse_square_root, 0, tiles, row_tile)
    paired = (own_rows.astype(jnp.float32) + partner.astype(jnp.float32)).astype(jnp.bfloat16)
    summed = lax.psum_scatter(paired, ("seq", "y"), scatter_dimension=0, tiled=True).astype(jnp.float32)
    own_rows = summed.shape[0]
    taps, c2 = w_dilated.shape[2], w_dilated.shape[3]
    split = residual_block_count * taps * c2
    return (
        output[None],
        upstream_gradient[None],
        summed[:, :split].reshape(own_rows, residual_block_count, taps, c2).transpose(1, 0, 2, 3),
        summed[:, split:].reshape(own_rows, residual_block_count, c2).transpose(1, 0, 2),
    )


def solution(mesh):
    win = mesh.shape["win"]
    grid = jax.sharding.Mesh(mesh.devices.reshape(mesh.shape["seq"], win // 2, 2), ALL)
    in_specs = (
        P(WIN, "seq", None),
        P(WIN, "seq", None),
        P(None, ALL, None, None),
        P(None, ALL, None),
        P(),
        P(),
        P(),
        P(),
    )
    out_specs = (
        P(WIN, "seq", None),
        P(WIN, "seq", None),
        P(None, ALL, None, None),
        P(None, ALL, None),
    )
    return jax.shard_map(
        per_device, mesh=grid, in_specs=in_specs, out_specs=out_specs, check_vma=False
    )
```

```python
import math

import jax
import jax.numpy as jnp
from jax import lax
from jax.experimental import pallas as pl
from jax.sharding import PartitionSpec as P

dilation_steps = (8, 16)
WIN = ("y", "core")
ALL = ("seq", "y", "core")


def padded_2(block, sides, width):
    for axis, dim in sides:
        count = lax.axis_size(axis)
        forward = [(i, i + 1) for i in range(count - 1)]
        backward = [(target, source) for source, target in forward]
        low = lax.ppermute(
            lax.slice_in_dim(block, block.shape[dim] - width, None, axis=dim), axis, forward
        )
        high = lax.ppermute(lax.slice_in_dim(block, 0, width, axis=dim), axis, backward)
        block = jnp.concatenate([low, block, high], axis=dim)
    return block


def gelu_value(values):
    return jax.nn.gelu(values, approximate=True)


def gelu_back(pre_values, upstream_gradient):
    return jax.vjp(gelu_value, pre_values)[1](upstream_gradient)[0]


def conv_forward_kernel(dilation, out_rows, act_ref, w_ref, scale_ref, shift_ref, out_ref):
    tap = pl.program_id(0)
    for kernel_tap in range(3):

        @pl.when(tap == kernel_tap)
        def _():
            lower = kernel_tap * dilation
            term = jnp.dot(
                act_ref[lower : lower + out_rows, :], w_ref[...], preferred_element_type=jnp.float32
            )
            if kernel_tap == 0:
                out_ref[...] = term
            elif kernel_tap == 1:
                out_ref[...] = out_ref[...] + term
            else:
                out_ref[...] = (out_ref[...] + term) * scale_ref[...] + shift_ref[...]


def conv_backward_kernel(dilation, out_rows, grad_ref, w_ref, out_ref):
    tap = pl.program_id(0)
    numbers = (((1,), (1,)), ((), ()))
    for kernel_tap in range(3):

        @pl.when(tap == kernel_tap)
        def _():
            lower = (2 - kernel_tap) * dilation
            term = lax.dot_general(
                grad_ref[lower : lower + out_rows, :],
                w_ref[...],
                numbers,
                preferred_element_type=jnp.float32,
            )
            if kernel_tap == 0:
                out_ref[...] = term
            else:
                out_ref[...] = out_ref[...] + term


def conv_forward(padded, gathered, block, c2, scale, shift, dilation, out_rows):
    rows = gathered.shape[0]
    return pl.pallas_call(
        lambda *refs: conv_forward_kernel(dilation, out_rows, *refs),
        grid=(3,),
        in_specs=[
            pl.BlockSpec(padded.shape, lambda k: (0, 0)),
            pl.BlockSpec((rows, c2), lambda k: (0, 3 * block + k)),
            pl.BlockSpec((1, c2), lambda k: (0, 0)),
            pl.BlockSpec((1, c2), lambda k: (0, 0)),
        ],
        out_specs=pl.BlockSpec((out_rows, c2), lambda k: (0, 0)),
        out_shape=jax.ShapeDtypeStruct((out_rows, c2), jnp.float32),
    )(padded, gathered, scale.reshape(1, c2), shift.reshape(1, c2))


def conv_backward(d_pad, gathered, block, c2, dilation, out_rows):
    rows = gathered.shape[0]
    return pl.pallas_call(
        lambda *refs: conv_backward_kernel(dilation, out_rows, *refs),
        grid=(3,),
        in_specs=[
            pl.BlockSpec(d_pad.shape, lambda k: (0, 0)),
            pl.BlockSpec((rows, c2), lambda k: (0, 3 * block + k)),
        ],
        out_specs=pl.BlockSpec((out_rows, rows), lambda k: (0, 0)),
        out_shape=jax.ShapeDtypeStruct((out_rows, rows), jnp.float32),
    )(d_pad, gathered)


def fetch_weights(w_dilated, w_mix):
    blocks, rows, taps, c2 = w_dilated.shape
    local = jnp.concatenate(
        [w_dilated.reshape(blocks, rows, taps * c2).transpose(1, 0, 2).reshape(rows, -1),
         w_mix.transpose(1, 0, 2).reshape(rows, -1)],
        axis=1,
    )
    gathered = lax.all_gather(local, ALL, axis=0, tiled=True)
    split = blocks * taps * c2
    return gathered, [gathered[:, split + b * c2 : split + (b + 1) * c2] for b in range(blocks)]


def shifted_taps(d_hidden, dilation):
    return jnp.concatenate(
        [jnp.pad(d_hidden, ((k * dilation, (2 - k) * dilation), (0, 0))) for k in range(3)], axis=1
    )


def gradient_kernel(scale, layout, count, *refs):
    out_ref = refs[-1]
    partner_refs = refs[2 * count : -1]
    for pair, (start, width, source, offset) in enumerate(layout):
        lhs = refs[2 * pair][...]
        rhs = refs[2 * pair + 1][...]
        term = (jnp.dot(lhs, rhs, preferred_element_type=jnp.float32) * scale).astype(out_ref.dtype)
        if source is not None:
            term = (
                term.astype(jnp.float32)
                + partner_refs[source][:, offset : offset + width].astype(jnp.float32)
            ).astype(out_ref.dtype)
        out_ref[:, start : start + width] = term


def weight_gradient_buffer(pairs, inverse_square_root, first_tile, tiles, partners=(), row_tile=256):
    widths = [rhs.shape[1] for _, rhs in pairs]
    layout = []
    start = 0
    for pair, width in enumerate(widths):
        if partners:
            source, offset = (0, start) if start < partners[0].shape[1] else (1, start - partners[0].shape[1])
        else:
            source, offset = None, 0
        layout.append((start, width, source, offset))
        start += width
    in_specs = []
    operands = []
    for lhs, rhs in pairs:
        in_specs.append(pl.BlockSpec((row_tile, lhs.shape[1]), lambda i: (i + first_tile, 0)))
        in_specs.append(pl.BlockSpec(rhs.shape, lambda i: (0, 0)))
        operands += [lhs, rhs]
    for partner in partners:
        in_specs.append(pl.BlockSpec((row_tile, partner.shape[1]), lambda i: (i, 0)))
        operands.append(partner)
    return pl.pallas_call(
        lambda *refs: gradient_kernel(inverse_square_root, tuple(layout), len(pairs), *refs),
        grid=(tiles,),
        in_specs=in_specs,
        out_specs=pl.BlockSpec((row_tile, start), lambda i: (i, 0)),
        out_shape=jax.ShapeDtypeStruct((tiles * row_tile, start), jnp.bfloat16),
    )(*operands)


def own_first(rows_by_channel):
    cores = lax.axis_size("core")
    core = lax.axis_index("core")
    grouped = rows_by_channel.reshape(-1, cores, rows_by_channel.shape[0] // (cores * lax.axis_size(("seq", "y"))), rows_by_channel.shape[1])
    order = (core + jnp.arange(cores)) % cores
    return jnp.take(grouped, order, axis=1).transpose(1, 0, 2, 3).reshape(rows_by_channel.shape)


def per_device(inputs, cotangent, w_dilated, w_mix, in_scale, in_shift, mid_scale, mid_shift):
    x_local = inputs[0]
    cot_local = cotangent[0]
    row_count = x_local.shape[0]
    window_len = lax.axis_size("seq") * row_count
    inverse_square_root = 1.0 / math.sqrt(lax.axis_size("y") * lax.axis_size("core") * inputs.shape[0] * window_len)
    residual_block_count = len(dilation_steps)
    saved = []
    gathered, mixing_weights = fetch_weights(w_dilated, w_mix)
    c2 = w_dilated.shape[3]
    remaining = sum(dilation_steps)
    first_row = lax.axis_index("seq") * row_count
    stream = padded_2(x_local, (("seq", 0),), remaining).astype(jnp.float32)
    for residual_block_index in range(residual_block_count):
        dilation = dilation_steps[residual_block_index]
        w_out = mixing_weights[residual_block_index]
        pre_in = stream * in_scale[residual_block_index] + in_shift[residual_block_index]
        position = first_row - remaining + lax.broadcasted_iota(jnp.int32, (pre_in.shape[0], 1), 0)
        inside = (position >= 0) & (position < window_len)
        activated = jnp.where(inside, gelu_value(pre_in), 0.0).astype(jnp.bfloat16)
        out_rows = row_count + 2 * (remaining - dilation)
        pre_mid = conv_forward(
            activated,
            gathered,
            residual_block_index,
            c2,
            mid_scale[residual_block_index],
            mid_shift[residual_block_index],
            dilation,
            out_rows,
        )
        middle = gelu_value(pre_mid).astype(jnp.bfloat16)
        stream = stream[dilation : dilation + out_rows] + jnp.einsum(
            "pe,ce->pc", middle, w_out, preferred_element_type=jnp.float32
        )
        own = remaining - dilation
        saved.append(
            (
                w_out,
                pre_in[remaining : remaining + row_count],
                activated[own : own + row_count + 2 * dilation],
                pre_mid[own : own + row_count],
                middle[own : own + row_count],
            )
        )
        remaining -= dilation
    output = stream.astype(jnp.bfloat16)
    upstream_gradient = cot_local.astype(jnp.float32)
    dilated_weight_gradients = [None] * residual_block_count
    partners = [None] * residual_block_count
    row_tile = 256
    mixing_weight_gradients = [None] * residual_block_count
    for residual_block_index in reversed(range(residual_block_count)):
        dilation = dilation_steps[residual_block_index]
        w_out, pre_in, padded, pre_mid, middle = saved[residual_block_index]
        cot_here = upstream_gradient.astype(jnp.bfloat16)
        d_mid = jnp.dot(cot_here, w_out, preferred_element_type=jnp.float32)
        d_hidden = (gelu_back(pre_mid, d_mid) * mid_scale[residual_block_index]).astype(
            jnp.bfloat16
        )
        d_pad = padded_2(d_hidden, (("seq", 0),), dilation)
        d_act = conv_backward(d_pad, gathered, residual_block_index, c2, dilation, row_count)
        dilated_weight_gradients[residual_block_index] = (own_first(padded.T), shifted_taps(d_hidden, dilation))
        mixing_weight_gradients[residual_block_index] = (own_first(cot_here.T), middle)
        block_pairs = [dilated_weight_gradients[residual_block_index], mixing_weight_gradients[residual_block_index]]
        tiles = padded.shape[1] // (row_tile * lax.axis_size("core"))
        partner_rows = weight_gradient_buffer(block_pairs, inverse_square_root, tiles, tiles, (), row_tile)
        partners[residual_block_index] = lax.ppermute(partner_rows, "core", [(0, 1), (1, 0)])
        upstream_gradient = (
            upstream_gradient + gelu_back(pre_in, d_act) * in_scale[residual_block_index]
        )
    pairs = [p for b in range(residual_block_count) for p in (dilated_weight_gradients[b], mixing_weight_gradients[b])]
    paired = weight_gradient_buffer(pairs, inverse_square_root, 0, tiles, tuple(partners), row_tile)
    summed = lax.psum_scatter(paired, ("seq", "y"), scatter_dimension=0, tiled=True).astype(jnp.float32)
    own_rows = summed.shape[0]
    taps, c2 = w_dilated.shape[2], w_dilated.shape[3]
    per_block = summed.reshape(own_rows, residual_block_count, (taps + 1) * c2).transpose(1, 0, 2)
    return (
        output[None],
        upstream_gradient[None],
        per_block[:, :, : taps * c2].reshape(residual_block_count, own_rows, taps, c2),
        per_block[:, :, taps * c2 :],
    )


def solution(mesh):
    win = mesh.shape["win"]
    grid = jax.sharding.Mesh(mesh.devices.reshape(mesh.shape["seq"], win // 2, 2), ALL)
    in_specs = (
        P(WIN, "seq", None),
        P(WIN, "seq", None),
        P(None, ALL, None, None),
        P(None, ALL, None),
        P(),
        P(),
        P(),
        P(),
    )
    out_specs = (
        P(WIN, "seq", None),
        P(WIN, "seq", None),
        P(None, ALL, None, None),
        P(None, ALL, None),
    )
    return jax.shard_map(
        per_device, mesh=grid, in_specs=in_specs, out_specs=out_specs, check_vma=False
    )
```

```python
import math

import jax
import jax.numpy as jnp
from jax import lax
from jax.experimental import pallas as pl
from jax.sharding import PartitionSpec as P

dilation_steps = (8, 16)
WIN = ("y", "core")
ALL = ("seq", "y", "core")


def padded_2(block, sides, width):
    for axis, dim in sides:
        count = lax.axis_size(axis)
        forward = [(i, i + 1) for i in range(count - 1)]
        backward = [(target, source) for source, target in forward]
        low = lax.ppermute(
            lax.slice_in_dim(block, block.shape[dim] - width, None, axis=dim), axis, forward
        )
        high = lax.ppermute(lax.slice_in_dim(block, 0, width, axis=dim), axis, backward)
        block = jnp.concatenate([low, block, high], axis=dim)
    return block


def gelu_value(values):
    return jax.nn.gelu(values, approximate=True)


def gelu_back(pre_values, upstream_gradient):
    return jax.vjp(gelu_value, pre_values)[1](upstream_gradient)[0]


def conv_forward_kernel(dilation, out_rows, act_ref, w_ref, scale_ref, shift_ref, out_ref):
    tap = pl.program_id(0)
    for kernel_tap in range(3):

        @pl.when(tap == kernel_tap)
        def _():
            lower = kernel_tap * dilation
            term = jnp.dot(
                act_ref[lower : lower + out_rows, :], w_ref[...], preferred_element_type=jnp.float32
            )
            if kernel_tap == 0:
                out_ref[...] = term
            elif kernel_tap == 1:
                out_ref[...] = out_ref[...] + term
            else:
                out_ref[...] = (out_ref[...] + term) * scale_ref[...] + shift_ref[...]


def conv_backward_kernel(dilation, out_rows, grad_ref, w_ref, out_ref):
    tap = pl.program_id(0)
    numbers = (((1,), (1,)), ((), ()))
    for kernel_tap in range(3):

        @pl.when(tap == kernel_tap)
        def _():
            lower = (2 - kernel_tap) * dilation
            term = lax.dot_general(
                grad_ref[lower : lower + out_rows, :],
                w_ref[...],
                numbers,
                preferred_element_type=jnp.float32,
            )
            if kernel_tap == 0:
                out_ref[...] = term
            else:
                out_ref[...] = out_ref[...] + term


def conv_forward(padded, gathered, block, c2, scale, shift, dilation, out_rows):
    rows = gathered.shape[0]
    return pl.pallas_call(
        lambda *refs: conv_forward_kernel(dilation, out_rows, *refs),
        grid=(3,),
        in_specs=[
            pl.BlockSpec(padded.shape, lambda k: (0, 0)),
            pl.BlockSpec((rows, c2), lambda k: (0, 3 * block + k)),
            pl.BlockSpec((1, c2), lambda k: (0, 0)),
            pl.BlockSpec((1, c2), lambda k: (0, 0)),
        ],
        out_specs=pl.BlockSpec((out_rows, c2), lambda k: (0, 0)),
        out_shape=jax.ShapeDtypeStruct((out_rows, c2), jnp.float32),
    )(padded, gathered, scale.reshape(1, c2), shift.reshape(1, c2))


def conv_backward(d_pad, gathered, block, c2, dilation, out_rows):
    rows = gathered.shape[0]
    return pl.pallas_call(
        lambda *refs: conv_backward_kernel(dilation, out_rows, *refs),
        grid=(3,),
        in_specs=[
            pl.BlockSpec(d_pad.shape, lambda k: (0, 0)),
            pl.BlockSpec((rows, c2), lambda k: (0, 3 * block + k)),
        ],
        out_specs=pl.BlockSpec((out_rows, rows), lambda k: (0, 0)),
        out_shape=jax.ShapeDtypeStruct((out_rows, rows), jnp.float32),
    )(d_pad, gathered)


def fetch_weights(w_dilated, w_mix):
    blocks, rows, taps, c2 = w_dilated.shape
    local = jnp.concatenate(
        [w_dilated.reshape(blocks, rows, taps * c2).transpose(1, 0, 2).reshape(rows, -1),
         w_mix.transpose(1, 0, 2).reshape(rows, -1)],
        axis=1,
    )
    gathered = lax.all_gather(local, ALL, axis=0, tiled=True)
    split = blocks * taps * c2
    return gathered, [gathered[:, split + b * c2 : split + (b + 1) * c2] for b in range(blocks)]


def shifted_taps(d_hidden, dilation):
    return jnp.concatenate(
        [jnp.pad(d_hidden, ((k * dilation, (2 - k) * dilation), (0, 0))) for k in range(3)], axis=1
    )


def gradient_kernel(scale, layout, count, has_partner, *refs):
    out_ref = refs[-1]
    partner_ref = refs[2 * count] if has_partner else None
    for pair, (start, width) in enumerate(layout):
        lhs = refs[2 * pair][...]
        rhs = refs[2 * pair + 1][...]
        term = (jnp.dot(lhs, rhs, preferred_element_type=jnp.float32) * scale).astype(out_ref.dtype)
        if has_partner:
            term = (
                term.astype(jnp.float32) + partner_ref[:, start : start + width].astype(jnp.float32)
            ).astype(out_ref.dtype)
        out_ref[:, start : start + width] = term


def weight_gradient_buffer(
    pairs, inverse_square_root, first_tile, tiles, partner=None, row_tile=256, column_block=0, into=None, blocks=1
):
    layout = []
    start = 0
    for _, rhs in pairs:
        layout.append((start, rhs.shape[1]))
        start += rhs.shape[1]
    in_specs = []
    operands = []
    for lhs, rhs in pairs:
        in_specs.append(pl.BlockSpec((row_tile, lhs.shape[1]), lambda i: (i + first_tile, 0)))
        in_specs.append(pl.BlockSpec(rhs.shape, lambda i: (0, 0)))
        operands += [lhs, rhs]
    if partner is not None:
        in_specs.append(pl.BlockSpec((row_tile, start), lambda i: (i, 0)))
        operands.append(partner)
    aliases = {}
    if into is not None:
        in_specs.append(pl.BlockSpec(memory_space=pl.ANY))
        operands.append(into)
        aliases = {len(operands) - 1: 0}
    return pl.pallas_call(
        lambda *refs: gradient_kernel(inverse_square_root, tuple(layout), len(pairs), partner is not None, *refs),
        grid=(tiles,),
        in_specs=in_specs,
        out_specs=pl.BlockSpec((row_tile, start), lambda i: (i, column_block)),
        out_shape=jax.ShapeDtypeStruct((tiles * row_tile, blocks * start), jnp.bfloat16),
        input_output_aliases=aliases,
    )(*operands)


def own_first(rows_by_channel):
    cores = lax.axis_size("core")
    core = lax.axis_index("core")
    grouped = rows_by_channel.reshape(-1, cores, rows_by_channel.shape[0] // (cores * lax.axis_size(("seq", "y"))), rows_by_channel.shape[1])
    order = (core + jnp.arange(cores)) % cores
    return jnp.take(grouped, order, axis=1).transpose(1, 0, 2, 3).reshape(rows_by_channel.shape)


def per_device(inputs, cotangent, w_dilated, w_mix, in_scale, in_shift, mid_scale, mid_shift):
    x_local = inputs[0]
    cot_local = cotangent[0]
    row_count = x_local.shape[0]
    window_len = lax.axis_size("seq") * row_count
    inverse_square_root = 1.0 / math.sqrt(lax.axis_size("y") * lax.axis_size("core") * inputs.shape[0] * window_len)
    residual_block_count = len(dilation_steps)
    saved = []
    gathered, mixing_weights = fetch_weights(w_dilated, w_mix)
    c2 = w_dilated.shape[3]
    remaining = sum(dilation_steps)
    first_row = lax.axis_index("seq") * row_count
    stream = padded_2(x_local, (("seq", 0),), remaining).astype(jnp.float32)
    for residual_block_index in range(residual_block_count):
        dilation = dilation_steps[residual_block_index]
        w_out = mixing_weights[residual_block_index]
        pre_in = stream * in_scale[residual_block_index] + in_shift[residual_block_index]
        position = first_row - remaining + lax.broadcasted_iota(jnp.int32, (pre_in.shape[0], 1), 0)
        inside = (position >= 0) & (position < window_len)
        activated = jnp.where(inside, gelu_value(pre_in), 0.0).astype(jnp.bfloat16)
        out_rows = row_count + 2 * (remaining - dilation)
        pre_mid = conv_forward(
            activated,
            gathered,
            residual_block_index,
            c2,
            mid_scale[residual_block_index],
            mid_shift[residual_block_index],
            dilation,
            out_rows,
        )
        middle = gelu_value(pre_mid).astype(jnp.bfloat16)
        stream = stream[dilation : dilation + out_rows] + jnp.einsum(
            "pe,ce->pc", middle, w_out, preferred_element_type=jnp.float32
        )
        own = remaining - dilation
        saved.append(
            (
                w_out,
                pre_in[remaining : remaining + row_count],
                activated[own : own + row_count + 2 * dilation],
                pre_mid[own : own + row_count],
                middle[own : own + row_count],
            )
        )
        remaining -= dilation
    output = stream.astype(jnp.bfloat16)
    upstream_gradient = cot_local.astype(jnp.float32)
    dilated_weight_gradients = [None] * residual_block_count
    partners = [None] * residual_block_count
    row_tile = 256
    mixing_weight_gradients = [None] * residual_block_count
    for residual_block_index in reversed(range(residual_block_count)):
        dilation = dilation_steps[residual_block_index]
        w_out, pre_in, padded, pre_mid, middle = saved[residual_block_index]
        cot_here = upstream_gradient.astype(jnp.bfloat16)
        d_mid = jnp.dot(cot_here, w_out, preferred_element_type=jnp.float32)
        d_hidden = (gelu_back(pre_mid, d_mid) * mid_scale[residual_block_index]).astype(
            jnp.bfloat16
        )
        d_pad = padded_2(d_hidden, (("seq", 0),), dilation)
        d_act = conv_backward(d_pad, gathered, residual_block_index, c2, dilation, row_count)
        dilated_weight_gradients[residual_block_index] = (own_first(padded.T), shifted_taps(d_hidden, dilation))
        mixing_weight_gradients[residual_block_index] = (own_first(cot_here.T), middle)
        block_pairs = [dilated_weight_gradients[residual_block_index], mixing_weight_gradients[residual_block_index]]
        tiles = padded.shape[1] // (row_tile * lax.axis_size("core"))
        partner_rows = weight_gradient_buffer(block_pairs, inverse_square_root, tiles, tiles, None, row_tile)
        partners[residual_block_index] = lax.ppermute(partner_rows, "core", [(0, 1), (1, 0)])
        upstream_gradient = (
            upstream_gradient + gelu_back(pre_in, d_act) * in_scale[residual_block_index]
        )
    paired = None
    for b in reversed(range(residual_block_count)):
        paired = weight_gradient_buffer(
            [dilated_weight_gradients[b], mixing_weight_gradients[b]],
            inverse_square_root,
            0,
            tiles,
            partners[b],
            row_tile,
            b,
            paired,
            residual_block_count,
        )
    summed = lax.psum_scatter(paired, ("seq", "y"), scatter_dimension=0, tiled=True).astype(jnp.float32)
    own_rows = summed.shape[0]
    taps, c2 = w_dilated.shape[2], w_dilated.shape[3]
    per_block = summed.reshape(own_rows, residual_block_count, (taps + 1) * c2).transpose(1, 0, 2)
    return (
        output[None],
        upstream_gradient[None],
        per_block[:, :, : taps * c2].reshape(residual_block_count, own_rows, taps, c2),
        per_block[:, :, taps * c2 :],
    )


def solution(mesh):
    win = mesh.shape["win"]
    grid = jax.sharding.Mesh(mesh.devices.reshape(mesh.shape["seq"], win // 2, 2), ALL)
    in_specs = (
        P(WIN, "seq", None),
        P(WIN, "seq", None),
        P(None, ALL, None, None),
        P(None, ALL, None),
        P(),
        P(),
        P(),
        P(),
    )
    out_specs = (
        P(WIN, "seq", None),
        P(WIN, "seq", None),
        P(None, ALL, None, None),
        P(None, ALL, None),
    )
    return jax.shard_map(
        per_device, mesh=grid, in_specs=in_specs, out_specs=out_specs, check_vma=False
    )
```

```python
import math

import jax
import jax.numpy as jnp
from jax import lax
from jax.experimental import pallas as pl
from jax.sharding import PartitionSpec as P

dilation_steps = (8, 16)
WIN = ("y", "core")
ALL = ("seq", "y", "core")


def padded_2(block, sides, width):
    for axis, dim in sides:
        count = lax.axis_size(axis)
        forward = [(i, i + 1) for i in range(count - 1)]
        backward = [(target, source) for source, target in forward]
        low = lax.ppermute(
            lax.slice_in_dim(block, block.shape[dim] - width, None, axis=dim), axis, forward
        )
        high = lax.ppermute(lax.slice_in_dim(block, 0, width, axis=dim), axis, backward)
        block = jnp.concatenate([low, block, high], axis=dim)
    return block


def gelu_value(values):
    return jax.nn.gelu(values, approximate=True)


def gelu_back(pre_values, upstream_gradient):
    return jax.vjp(gelu_value, pre_values)[1](upstream_gradient)[0]


def conv_forward_kernel(dilation, out_rows, act_ref, w_ref, scale_ref, shift_ref, out_ref):
    tap = pl.program_id(0)
    for kernel_tap in range(3):

        @pl.when(tap == kernel_tap)
        def _():
            lower = kernel_tap * dilation
            term = jnp.dot(
                act_ref[lower : lower + out_rows, :], w_ref[...], preferred_element_type=jnp.float32
            )
            if kernel_tap == 0:
                out_ref[...] = term
            elif kernel_tap == 1:
                out_ref[...] = out_ref[...] + term
            else:
                out_ref[...] = (out_ref[...] + term) * scale_ref[...] + shift_ref[...]


def conv_backward_kernel(dilation, out_rows, grad_ref, w_ref, out_ref):
    tap = pl.program_id(0)
    numbers = (((1,), (1,)), ((), ()))
    for kernel_tap in range(3):

        @pl.when(tap == kernel_tap)
        def _():
            lower = (2 - kernel_tap) * dilation
            term = lax.dot_general(
                grad_ref[lower : lower + out_rows, :],
                w_ref[...],
                numbers,
                preferred_element_type=jnp.float32,
            )
            if kernel_tap == 0:
                out_ref[...] = term
            else:
                out_ref[...] = out_ref[...] + term


def conv_forward(padded, gathered, block, c2, scale, shift, dilation, out_rows):
    rows = gathered.shape[0]
    return pl.pallas_call(
        lambda *refs: conv_forward_kernel(dilation, out_rows, *refs),
        grid=(3,),
        in_specs=[
            pl.BlockSpec(padded.shape, lambda k: (0, 0)),
            pl.BlockSpec((rows, c2), lambda k: (0, 3 * block + k)),
            pl.BlockSpec((1, c2), lambda k: (0, 0)),
            pl.BlockSpec((1, c2), lambda k: (0, 0)),
        ],
        out_specs=pl.BlockSpec((out_rows, c2), lambda k: (0, 0)),
        out_shape=jax.ShapeDtypeStruct((out_rows, c2), jnp.float32),
    )(padded, gathered, scale.reshape(1, c2), shift.reshape(1, c2))


def conv_backward(d_pad, gathered, block, c2, dilation, out_rows):
    rows = gathered.shape[0]
    return pl.pallas_call(
        lambda *refs: conv_backward_kernel(dilation, out_rows, *refs),
        grid=(3,),
        in_specs=[
            pl.BlockSpec(d_pad.shape, lambda k: (0, 0)),
            pl.BlockSpec((rows, c2), lambda k: (0, 3 * block + k)),
        ],
        out_specs=pl.BlockSpec((out_rows, rows), lambda k: (0, 0)),
        out_shape=jax.ShapeDtypeStruct((out_rows, rows), jnp.float32),
    )(d_pad, gathered)


def fetch_weights(w_dilated, w_mix):
    blocks, rows, taps, c2 = w_dilated.shape
    local = jnp.concatenate(
        [w_dilated.reshape(blocks, rows, taps * c2).transpose(1, 0, 2).reshape(rows, -1),
         w_mix.transpose(1, 0, 2).reshape(rows, -1)],
        axis=1,
    )
    gathered = lax.all_gather(local, ALL, axis=0, tiled=True)
    split = blocks * taps * c2
    return gathered, [gathered[:, split + b * c2 : split + (b + 1) * c2] for b in range(blocks)]


def shifted_taps(d_hidden, dilation):
    return jnp.concatenate(
        [jnp.pad(d_hidden, ((k * dilation, (2 - k) * dilation), (0, 0))) for k in range(3)], axis=1
    )


def gradient_kernel(scale, layout, count, has_partner, *refs):
    out_ref = refs[-1]
    partner_ref = refs[2 * count] if has_partner else None
    for pair, (start, width) in enumerate(layout):
        lhs = refs[2 * pair][...]
        rhs = refs[2 * pair + 1][...]
        term = (jnp.dot(lhs, rhs, preferred_element_type=jnp.float32) * scale).astype(out_ref.dtype)
        if has_partner:
            term = (
                term.astype(jnp.float32) + partner_ref[:, start : start + width].astype(jnp.float32)
            ).astype(out_ref.dtype)
        out_ref[:, start : start + width] = term


def weight_gradient_buffer(
    pairs, inverse_square_root, first_tile, tiles, partner=None, row_tile=256, column_block=0, into=None, blocks=1
):
    layout = []
    start = 0
    for _, rhs in pairs:
        layout.append((start, rhs.shape[1]))
        start += rhs.shape[1]
    in_specs = []
    operands = []
    for lhs, rhs in pairs:
        in_specs.append(pl.BlockSpec((row_tile, lhs.shape[1]), lambda i: (i + first_tile, 0)))
        in_specs.append(pl.BlockSpec(rhs.shape, lambda i: (0, 0)))
        operands += [lhs, rhs]
    if partner is not None:
        in_specs.append(pl.BlockSpec((row_tile, start), lambda i: (i, 0)))
        operands.append(partner)
    aliases = {}
    if into is not None:
        in_specs.append(pl.BlockSpec(memory_space=pl.ANY))
        operands.append(into)
        aliases = {len(operands) - 1: 0}
    return pl.pallas_call(
        lambda *refs: gradient_kernel(inverse_square_root, tuple(layout), len(pairs), partner is not None, *refs),
        grid=(tiles,),
        in_specs=in_specs,
        out_specs=pl.BlockSpec((row_tile, start), lambda i: (i, column_block)),
        out_shape=jax.ShapeDtypeStruct((tiles * row_tile, blocks * start), jnp.bfloat16),
        input_output_aliases=aliases,
    )(*operands)


def own_first(rows_by_channel):
    cores = lax.axis_size("core")
    core = lax.axis_index("core")
    grouped = rows_by_channel.reshape(-1, cores, rows_by_channel.shape[0] // (cores * lax.axis_size(("seq", "y"))), rows_by_channel.shape[1])
    order = (core + jnp.arange(cores)) % cores
    return jnp.take(grouped, order, axis=1).transpose(1, 0, 2, 3).reshape(rows_by_channel.shape)


def per_device(inputs, cotangent, w_dilated, w_mix, in_scale, in_shift, mid_scale, mid_shift):
    x_local = inputs[0]
    cot_local = cotangent[0]
    row_count = x_local.shape[0]
    window_len = lax.axis_size("seq") * row_count
    inverse_square_root = 1.0 / math.sqrt(lax.axis_size("y") * lax.axis_size("core") * inputs.shape[0] * window_len)
    residual_block_count = len(dilation_steps)
    saved = []
    gathered, mixing_weights = fetch_weights(w_dilated, w_mix)
    c2 = w_dilated.shape[3]
    remaining = sum(dilation_steps)
    first_row = lax.axis_index("seq") * row_count
    stream = padded_2(x_local, (("seq", 0),), remaining).astype(jnp.float32)
    for residual_block_index in range(residual_block_count):
        dilation = dilation_steps[residual_block_index]
        w_out = mixing_weights[residual_block_index]
        pre_in = stream * in_scale[residual_block_index] + in_shift[residual_block_index]
        position = first_row - remaining + lax.broadcasted_iota(jnp.int32, (pre_in.shape[0], 1), 0)
        inside = (position >= 0) & (position < window_len)
        activated = jnp.where(inside, gelu_value(pre_in), 0.0).astype(jnp.bfloat16)
        out_rows = row_count + 2 * (remaining - dilation)
        pre_mid = conv_forward(
            activated,
            gathered,
            residual_block_index,
            c2,
            mid_scale[residual_block_index],
            mid_shift[residual_block_index],
            dilation,
            out_rows,
        )
        middle = gelu_value(pre_mid).astype(jnp.bfloat16)
        stream = stream[dilation : dilation + out_rows] + jnp.einsum(
            "pe,ce->pc", middle, w_out, preferred_element_type=jnp.float32
        )
        own = remaining - dilation
        saved.append(
            (
                w_out,
                pre_in[remaining : remaining + row_count],
                activated[own : own + row_count + 2 * dilation],
                pre_mid[own : own + row_count],
                middle[own : own + row_count],
            )
        )
        remaining -= dilation
    output = stream.astype(jnp.bfloat16)
    upstream_gradient = cot_local.astype(jnp.float32)
    dilated_weight_gradients = [None] * residual_block_count
    partners = [None] * residual_block_count
    row_tile = 384
    mixing_weight_gradients = [None] * residual_block_count
    for residual_block_index in reversed(range(residual_block_count)):
        dilation = dilation_steps[residual_block_index]
        w_out, pre_in, padded, pre_mid, middle = saved[residual_block_index]
        cot_here = upstream_gradient.astype(jnp.bfloat16)
        d_mid = jnp.dot(cot_here, w_out, preferred_element_type=jnp.float32)
        d_hidden = (gelu_back(pre_mid, d_mid) * mid_scale[residual_block_index]).astype(
            jnp.bfloat16
        )
        d_pad = padded_2(d_hidden, (("seq", 0),), dilation)
        d_act = conv_backward(d_pad, gathered, residual_block_index, c2, dilation, row_count)
        dilated_weight_gradients[residual_block_index] = (own_first(padded.T), shifted_taps(d_hidden, dilation))
        mixing_weight_gradients[residual_block_index] = (own_first(cot_here.T), middle)
        block_pairs = [dilated_weight_gradients[residual_block_index], mixing_weight_gradients[residual_block_index]]
        tiles = padded.shape[1] // (row_tile * lax.axis_size("core"))
        partner_rows = weight_gradient_buffer(block_pairs, inverse_square_root, tiles, tiles, None, row_tile)
        partners[residual_block_index] = lax.ppermute(partner_rows, "core", [(0, 1), (1, 0)])
        upstream_gradient = (
            upstream_gradient + gelu_back(pre_in, d_act) * in_scale[residual_block_index]
        )
    paired = None
    for b in reversed(range(residual_block_count)):
        paired = weight_gradient_buffer(
            [dilated_weight_gradients[b], mixing_weight_gradients[b]],
            inverse_square_root,
            0,
            tiles,
            partners[b],
            row_tile,
            b,
            paired,
            residual_block_count,
        )
    summed = lax.psum_scatter(paired, ("seq", "y"), scatter_dimension=0, tiled=True).astype(jnp.float32)
    own_rows = summed.shape[0]
    taps, c2 = w_dilated.shape[2], w_dilated.shape[3]
    per_block = summed.reshape(own_rows, residual_block_count, (taps + 1) * c2).transpose(1, 0, 2)
    return (
        output[None],
        upstream_gradient[None],
        per_block[:, :, : taps * c2].reshape(residual_block_count, own_rows, taps, c2),
        per_block[:, :, taps * c2 :],
    )


def solution(mesh):
    win = mesh.shape["win"]
    grid = jax.sharding.Mesh(mesh.devices.reshape(mesh.shape["seq"], win // 2, 2), ALL)
    in_specs = (
        P(WIN, "seq", None),
        P(WIN, "seq", None),
        P(None, ALL, None, None),
        P(None, ALL, None),
        P(),
        P(),
        P(),
        P(),
    )
    out_specs = (
        P(WIN, "seq", None),
        P(WIN, "seq", None),
        P(None, ALL, None, None),
        P(None, ALL, None),
    )
    return jax.shard_map(
        per_device, mesh=grid, in_specs=in_specs, out_specs=out_specs, check_vma=False
    )
```

```python
import math

import jax
import jax.numpy as jnp
from jax import lax
from jax.experimental import pallas as pl
from jax.sharding import PartitionSpec as P

dilation_steps = (8, 16)
WIN = ("y", "core")
ALL = ("seq", "y", "core")


def padded_2(block, sides, width):
    for axis, dim in sides:
        count = lax.axis_size(axis)
        forward = [(i, i + 1) for i in range(count - 1)]
        backward = [(target, source) for source, target in forward]
        low = lax.ppermute(
            lax.slice_in_dim(block, block.shape[dim] - width, None, axis=dim), axis, forward
        )
        high = lax.ppermute(lax.slice_in_dim(block, 0, width, axis=dim), axis, backward)
        block = jnp.concatenate([low, block, high], axis=dim)
    return block


def gelu_value(values):
    return jax.nn.gelu(values, approximate=True)


def gelu_back(pre_values, upstream_gradient):
    return jax.vjp(gelu_value, pre_values)[1](upstream_gradient)[0]


def conv_forward_kernel(dilation, out_rows, act_ref, w_ref, scale_ref, shift_ref, out_ref):
    tap = pl.program_id(0)
    for kernel_tap in range(3):

        @pl.when(tap == kernel_tap)
        def _():
            lower = kernel_tap * dilation
            term = jnp.dot(
                act_ref[lower : lower + out_rows, :], w_ref[...], preferred_element_type=jnp.float32
            )
            if kernel_tap == 0:
                out_ref[...] = term
            elif kernel_tap == 1:
                out_ref[...] = out_ref[...] + term
            else:
                out_ref[...] = (out_ref[...] + term) * scale_ref[...] + shift_ref[...]


def conv_backward_kernel(dilation, out_rows, grad_ref, w_ref, out_ref):
    tap = pl.program_id(0)
    numbers = (((1,), (1,)), ((), ()))
    for kernel_tap in range(3):

        @pl.when(tap == kernel_tap)
        def _():
            lower = (2 - kernel_tap) * dilation
            term = lax.dot_general(
                grad_ref[lower : lower + out_rows, :],
                w_ref[...],
                numbers,
                preferred_element_type=jnp.float32,
            )
            if kernel_tap == 0:
                out_ref[...] = term
            else:
                out_ref[...] = out_ref[...] + term


def conv_forward(padded, gathered, block, c2, scale, shift, dilation, out_rows):
    rows = gathered.shape[0]
    return pl.pallas_call(
        lambda *refs: conv_forward_kernel(dilation, out_rows, *refs),
        grid=(3,),
        in_specs=[
            pl.BlockSpec(padded.shape, lambda k: (0, 0)),
            pl.BlockSpec((rows, c2), lambda k: (0, 3 * block + k)),
            pl.BlockSpec((1, c2), lambda k: (0, 0)),
            pl.BlockSpec((1, c2), lambda k: (0, 0)),
        ],
        out_specs=pl.BlockSpec((out_rows, c2), lambda k: (0, 0)),
        out_shape=jax.ShapeDtypeStruct((out_rows, c2), jnp.float32),
    )(padded, gathered, scale.reshape(1, c2), shift.reshape(1, c2))


def conv_backward(d_pad, gathered, block, c2, dilation, out_rows):
    rows = gathered.shape[0]
    return pl.pallas_call(
        lambda *refs: conv_backward_kernel(dilation, out_rows, *refs),
        grid=(3,),
        in_specs=[
            pl.BlockSpec(d_pad.shape, lambda k: (0, 0)),
            pl.BlockSpec((rows, c2), lambda k: (0, 3 * block + k)),
        ],
        out_specs=pl.BlockSpec((out_rows, rows), lambda k: (0, 0)),
        out_shape=jax.ShapeDtypeStruct((out_rows, rows), jnp.float32),
    )(d_pad, gathered)


def fetch_weights(w_dilated, w_mix):
    blocks, rows, taps, c2 = w_dilated.shape
    local = jnp.concatenate(
        [w_dilated.reshape(blocks, rows, taps * c2).transpose(1, 0, 2).reshape(rows, -1),
         w_mix.transpose(1, 0, 2).reshape(rows, -1)],
        axis=1,
    )
    gathered = lax.all_gather(local, ALL, axis=0, tiled=True)
    split = blocks * taps * c2
    return gathered, [gathered[:, split + b * c2 : split + (b + 1) * c2] for b in range(blocks)]


def shifted_taps(d_hidden, dilation):
    return jnp.concatenate(
        [jnp.pad(d_hidden, ((k * dilation, (2 - k) * dilation), (0, 0))) for k in range(3)], axis=1
    )


def gradient_kernel(scale, layout, count, has_partner, *refs):
    out_ref = refs[-1]
    partner_ref = refs[2 * count] if has_partner else None
    for pair, (start, width) in enumerate(layout):
        lhs = refs[2 * pair][...]
        rhs = refs[2 * pair + 1][...]
        term = (jnp.dot(lhs, rhs, preferred_element_type=jnp.float32) * scale).astype(out_ref.dtype)
        if has_partner:
            term = (
                term.astype(jnp.float32) + partner_ref[:, start : start + width].astype(jnp.float32)
            ).astype(out_ref.dtype)
        out_ref[:, start : start + width] = term


def weight_gradient_buffer(
    pairs, inverse_square_root, first_tile, tiles, partner=None, row_tile=256, column_block=0, into=None, blocks=1
):
    layout = []
    start = 0
    for _, rhs in pairs:
        layout.append((start, rhs.shape[1]))
        start += rhs.shape[1]
    in_specs = []
    operands = []
    for lhs, rhs in pairs:
        in_specs.append(pl.BlockSpec((row_tile, lhs.shape[1]), lambda i: (i + first_tile, 0)))
        in_specs.append(pl.BlockSpec(rhs.shape, lambda i: (0, 0)))
        operands += [lhs, rhs]
    if partner is not None:
        in_specs.append(pl.BlockSpec((row_tile, start), lambda i: (i, 0)))
        operands.append(partner)
    aliases = {}
    if into is not None:
        in_specs.append(pl.BlockSpec(memory_space=pl.ANY))
        operands.append(into)
        aliases = {len(operands) - 1: 0}
    return pl.pallas_call(
        lambda *refs: gradient_kernel(inverse_square_root, tuple(layout), len(pairs), partner is not None, *refs),
        grid=(tiles,),
        in_specs=in_specs,
        out_specs=pl.BlockSpec((row_tile, start), lambda i: (i, column_block)),
        out_shape=jax.ShapeDtypeStruct((tiles * row_tile, blocks * start), jnp.bfloat16),
        input_output_aliases=aliases,
    )(*operands)


def own_first(rows_by_channel):
    cores = lax.axis_size("core")
    core = lax.axis_index("core")
    grouped = rows_by_channel.reshape(-1, cores, rows_by_channel.shape[0] // (cores * lax.axis_size(("seq", "y"))), rows_by_channel.shape[1])
    order = (core + jnp.arange(cores)) % cores
    return jnp.take(grouped, order, axis=1).transpose(1, 0, 2, 3).reshape(rows_by_channel.shape)


def per_device(inputs, cotangent, w_dilated, w_mix, in_scale, in_shift, mid_scale, mid_shift):
    x_local = inputs[0]
    cot_local = cotangent[0]
    row_count = x_local.shape[0]
    window_len = lax.axis_size("seq") * row_count
    inverse_square_root = 1.0 / math.sqrt(lax.axis_size("y") * lax.axis_size("core") * inputs.shape[0] * window_len)
    residual_block_count = len(dilation_steps)
    saved = []
    gathered, mixing_weights = fetch_weights(w_dilated, w_mix)
    c2 = w_dilated.shape[3]
    remaining = sum(dilation_steps)
    first_row = lax.axis_index("seq") * row_count
    stream = padded_2(x_local, (("seq", 0),), remaining).astype(jnp.float32)
    for residual_block_index in range(residual_block_count):
        dilation = dilation_steps[residual_block_index]
        w_out = mixing_weights[residual_block_index]
        pre_in = stream * in_scale[residual_block_index] + in_shift[residual_block_index]
        position = first_row - remaining + lax.broadcasted_iota(jnp.int32, (pre_in.shape[0], 1), 0)
        inside = (position >= 0) & (position < window_len)
        activated = jnp.where(inside, gelu_value(pre_in), 0.0).astype(jnp.bfloat16)
        out_rows = row_count + 2 * (remaining - dilation)
        pre_mid = conv_forward(
            activated,
            gathered,
            residual_block_index,
            c2,
            mid_scale[residual_block_index],
            mid_shift[residual_block_index],
            dilation,
            out_rows,
        )
        middle = gelu_value(pre_mid).astype(jnp.bfloat16)
        stream = stream[dilation : dilation + out_rows] + jnp.einsum(
            "pe,ce->pc", middle, w_out, preferred_element_type=jnp.float32
        )
        own = remaining - dilation
        saved.append(
            (
                w_out,
                pre_in[remaining : remaining + row_count],
                activated[own : own + row_count + 2 * dilation],
                pre_mid[own : own + row_count],
                middle[own : own + row_count],
            )
        )
        remaining -= dilation
    output = stream.astype(jnp.bfloat16)
    upstream_gradient = cot_local.astype(jnp.float32)
    dilated_weight_gradients = [None] * residual_block_count
    partners = [None] * residual_block_count
    row_tile = 768
    mixing_weight_gradients = [None] * residual_block_count
    for residual_block_index in reversed(range(residual_block_count)):
        dilation = dilation_steps[residual_block_index]
        w_out, pre_in, padded, pre_mid, middle = saved[residual_block_index]
        cot_here = upstream_gradient.astype(jnp.bfloat16)
        d_mid = jnp.dot(cot_here, w_out, preferred_element_type=jnp.float32)
        d_hidden = (gelu_back(pre_mid, d_mid) * mid_scale[residual_block_index]).astype(
            jnp.bfloat16
        )
        d_pad = padded_2(d_hidden, (("seq", 0),), dilation)
        d_act = conv_backward(d_pad, gathered, residual_block_index, c2, dilation, row_count)
        dilated_weight_gradients[residual_block_index] = (own_first(padded.T), shifted_taps(d_hidden, dilation))
        mixing_weight_gradients[residual_block_index] = (own_first(cot_here.T), middle)
        block_pairs = [dilated_weight_gradients[residual_block_index], mixing_weight_gradients[residual_block_index]]
        tiles = padded.shape[1] // (row_tile * lax.axis_size("core"))
        partner_rows = weight_gradient_buffer(block_pairs, inverse_square_root, tiles, tiles, None, row_tile)
        partners[residual_block_index] = lax.ppermute(partner_rows, "core", [(0, 1), (1, 0)])
        upstream_gradient = (
            upstream_gradient + gelu_back(pre_in, d_act) * in_scale[residual_block_index]
        )
    paired = None
    for b in reversed(range(residual_block_count)):
        paired = weight_gradient_buffer(
            [dilated_weight_gradients[b], mixing_weight_gradients[b]],
            inverse_square_root,
            0,
            tiles,
            partners[b],
            row_tile,
            b,
            paired,
            residual_block_count,
        )
    summed = lax.psum_scatter(paired, ("seq", "y"), scatter_dimension=0, tiled=True).astype(jnp.float32)
    own_rows = summed.shape[0]
    taps, c2 = w_dilated.shape[2], w_dilated.shape[3]
    per_block = summed.reshape(own_rows, residual_block_count, (taps + 1) * c2).transpose(1, 0, 2)
    return (
        output[None],
        upstream_gradient[None],
        per_block[:, :, : taps * c2].reshape(residual_block_count, own_rows, taps, c2),
        per_block[:, :, taps * c2 :],
    )


def solution(mesh):
    win = mesh.shape["win"]
    grid = jax.sharding.Mesh(mesh.devices.reshape(mesh.shape["seq"], win // 2, 2), ALL)
    in_specs = (
        P(WIN, "seq", None),
        P(WIN, "seq", None),
        P(None, ALL, None, None),
        P(None, ALL, None),
        P(),
        P(),
        P(),
        P(),
    )
    out_specs = (
        P(WIN, "seq", None),
        P(WIN, "seq", None),
        P(None, ALL, None, None),
        P(None, ALL, None),
    )
    return jax.shard_map(
        per_device, mesh=grid, in_specs=in_specs, out_specs=out_specs, check_vma=False
    )
```

```python
import math

import jax
import jax.numpy as jnp
from jax import lax
from jax.experimental import pallas as pl
from jax.sharding import PartitionSpec as P

dilation_steps = (8, 16)
WIN = ("y", "core")
ALL = ("seq", "y", "core")


def padded_2(block, sides, width):
    for axis, dim in sides:
        count = lax.axis_size(axis)
        forward = [(i, i + 1) for i in range(count - 1)]
        backward = [(target, source) for source, target in forward]
        low = lax.ppermute(
            lax.slice_in_dim(block, block.shape[dim] - width, None, axis=dim), axis, forward
        )
        high = lax.ppermute(lax.slice_in_dim(block, 0, width, axis=dim), axis, backward)
        block = jnp.concatenate([low, block, high], axis=dim)
    return block


def gelu_value(values):
    return jax.nn.gelu(values, approximate=True)


def gelu_back(pre_values, upstream_gradient):
    return jax.vjp(gelu_value, pre_values)[1](upstream_gradient)[0]


def conv_forward_kernel(dilation, out_rows, act_ref, w_ref, scale_ref, shift_ref, out_ref):
    tap = pl.program_id(0)
    for kernel_tap in range(3):

        @pl.when(tap == kernel_tap)
        def _():
            lower = kernel_tap * dilation
            term = jnp.dot(
                act_ref[lower : lower + out_rows, :], w_ref[...], preferred_element_type=jnp.float32
            )
            if kernel_tap == 0:
                out_ref[...] = term
            elif kernel_tap == 1:
                out_ref[...] = out_ref[...] + term
            else:
                out_ref[...] = (out_ref[...] + term) * scale_ref[...] + shift_ref[...]


def conv_backward_kernel(dilation, out_rows, grad_ref, w_ref, out_ref):
    tap = pl.program_id(0)
    numbers = (((1,), (1,)), ((), ()))
    for kernel_tap in range(3):

        @pl.when(tap == kernel_tap)
        def _():
            lower = (2 - kernel_tap) * dilation
            term = lax.dot_general(
                grad_ref[lower : lower + out_rows, :],
                w_ref[...],
                numbers,
                preferred_element_type=jnp.float32,
            )
            if kernel_tap == 0:
                out_ref[...] = term
            else:
                out_ref[...] = out_ref[...] + term


def conv_forward(padded, gathered, block, c2, scale, shift, dilation, out_rows):
    rows = gathered.shape[0]
    return pl.pallas_call(
        lambda *refs: conv_forward_kernel(dilation, out_rows, *refs),
        grid=(3,),
        in_specs=[
            pl.BlockSpec(padded.shape, lambda k: (0, 0)),
            pl.BlockSpec((rows, c2), lambda k: (0, 3 * block + k)),
            pl.BlockSpec((1, c2), lambda k: (0, 0)),
            pl.BlockSpec((1, c2), lambda k: (0, 0)),
        ],
        out_specs=pl.BlockSpec((out_rows, c2), lambda k: (0, 0)),
        out_shape=jax.ShapeDtypeStruct((out_rows, c2), jnp.float32),
    )(padded, gathered, scale.reshape(1, c2), shift.reshape(1, c2))


def conv_backward(d_pad, gathered, block, c2, dilation, out_rows):
    rows = gathered.shape[0]
    return pl.pallas_call(
        lambda *refs: conv_backward_kernel(dilation, out_rows, *refs),
        grid=(3,),
        in_specs=[
            pl.BlockSpec(d_pad.shape, lambda k: (0, 0)),
            pl.BlockSpec((rows, c2), lambda k: (0, 3 * block + k)),
        ],
        out_specs=pl.BlockSpec((out_rows, rows), lambda k: (0, 0)),
        out_shape=jax.ShapeDtypeStruct((out_rows, rows), jnp.float32),
    )(d_pad, gathered)


def fetch_weights(w_dilated, w_mix):
    blocks, rows, taps, c2 = w_dilated.shape
    local = jnp.concatenate(
        [w_dilated.reshape(blocks, rows, taps * c2).transpose(1, 0, 2).reshape(rows, -1),
         w_mix.transpose(1, 0, 2).reshape(rows, -1)],
        axis=1,
    )
    gathered = lax.all_gather(local, ALL, axis=0, tiled=True)
    split = blocks * taps * c2
    return gathered, [gathered[:, split + b * c2 : split + (b + 1) * c2] for b in range(blocks)]


def shifted_taps(d_hidden, dilation):
    return jnp.concatenate(
        [jnp.pad(d_hidden, ((k * dilation, (2 - k) * dilation), (0, 0))) for k in range(3)], axis=1
    )


def gradient_kernel(scale, layout, count, has_partner, *refs):
    out_ref = refs[-1]
    partner_ref = refs[2 * count] if has_partner else None
    for pair, (start, width) in enumerate(layout):
        lhs = refs[2 * pair][...]
        rhs = refs[2 * pair + 1][...]
        term = (jnp.dot(lhs, rhs, preferred_element_type=jnp.float32) * scale).astype(out_ref.dtype)
        if has_partner:
            term = (
                term.astype(jnp.float32) + partner_ref[:, start : start + width].astype(jnp.float32)
            ).astype(out_ref.dtype)
        out_ref[:, start : start + width] = term


def weight_gradient_buffer(
    pairs, inverse_square_root, first_tile, tiles, partner=None, row_tile=256, column_block=0, into=None, blocks=1
):
    layout = []
    start = 0
    for _, rhs in pairs:
        layout.append((start, rhs.shape[1]))
        start += rhs.shape[1]
    in_specs = []
    operands = []
    for lhs, rhs in pairs:
        in_specs.append(pl.BlockSpec((row_tile, lhs.shape[1]), lambda i: (i + first_tile, 0)))
        in_specs.append(pl.BlockSpec(rhs.shape, lambda i: (0, 0)))
        operands += [lhs, rhs]
    if partner is not None:
        in_specs.append(pl.BlockSpec((row_tile, start), lambda i: (i, 0)))
        operands.append(partner)
    aliases = {}
    if into is not None:
        in_specs.append(pl.BlockSpec(memory_space=pl.ANY))
        operands.append(into)
        aliases = {len(operands) - 1: 0}
    return pl.pallas_call(
        lambda *refs: gradient_kernel(inverse_square_root, tuple(layout), len(pairs), partner is not None, *refs),
        grid=(tiles,),
        in_specs=in_specs,
        out_specs=pl.BlockSpec((row_tile, start), lambda i: (i, column_block)),
        out_shape=jax.ShapeDtypeStruct((tiles * row_tile, blocks * start), jnp.bfloat16),
        input_output_aliases=aliases,
    )(*operands)


def own_first(rows_by_channel):
    cores = lax.axis_size("core")
    core = lax.axis_index("core")
    grouped = rows_by_channel.reshape(-1, cores, rows_by_channel.shape[0] // (cores * lax.axis_size(("seq", "y"))), rows_by_channel.shape[1])
    order = (core + jnp.arange(cores)) % cores
    return jnp.take(grouped, order, axis=1).transpose(1, 0, 2, 3).reshape(rows_by_channel.shape)


def per_device(inputs, cotangent, w_dilated, w_mix, in_scale, in_shift, mid_scale, mid_shift):
    x_local = inputs[0]
    cot_local = cotangent[0]
    row_count = x_local.shape[0]
    window_len = lax.axis_size("seq") * row_count
    inverse_square_root = 1.0 / math.sqrt(lax.axis_size("y") * lax.axis_size("core") * inputs.shape[0] * window_len)
    residual_block_count = len(dilation_steps)
    saved = []
    gathered, mixing_weights = fetch_weights(w_dilated, w_mix)
    c2 = w_dilated.shape[3]
    remaining = sum(dilation_steps)
    first_row = lax.axis_index("seq") * row_count
    stream = padded_2(x_local, (("seq", 0),), remaining).astype(jnp.float32)
    for residual_block_index in range(residual_block_count):
        dilation = dilation_steps[residual_block_index]
        w_out = mixing_weights[residual_block_index]
        pre_in = stream * in_scale[residual_block_index] + in_shift[residual_block_index]
        position = first_row - remaining + lax.broadcasted_iota(jnp.int32, (pre_in.shape[0], 1), 0)
        inside = (position >= 0) & (position < window_len)
        activated = jnp.where(inside, gelu_value(pre_in), 0.0).astype(jnp.bfloat16)
        out_rows = row_count + 2 * (remaining - dilation)
        pre_mid = conv_forward(
            activated,
            gathered,
            residual_block_index,
            c2,
            mid_scale[residual_block_index],
            mid_shift[residual_block_index],
            dilation,
            out_rows,
        )
        middle = gelu_value(pre_mid).astype(jnp.bfloat16)
        stream = stream[dilation : dilation + out_rows] + jnp.einsum(
            "pe,ce->pc", middle, w_out, preferred_element_type=jnp.float32
        )
        own = remaining - dilation
        saved.append(
            (
                w_out,
                pre_in[remaining : remaining + row_count],
                activated[own : own + row_count + 2 * dilation],
                pre_mid[own : own + row_count],
                middle[own : own + row_count],
            )
        )
        remaining -= dilation
    output = stream.astype(jnp.bfloat16)
    upstream_gradient = cot_local.astype(jnp.float32)
    dilated_weight_gradients = [None] * residual_block_count
    partners = [None] * residual_block_count
    row_tile = 384
    mixing_weight_gradients = [None] * residual_block_count
    for residual_block_index in reversed(range(residual_block_count)):
        dilation = dilation_steps[residual_block_index]
        w_out, pre_in, padded, pre_mid, middle = saved[residual_block_index]
        cot_here = upstream_gradient.astype(jnp.bfloat16)
        d_mid = jnp.dot(cot_here, w_out, preferred_element_type=jnp.float32)
        d_hidden = (gelu_back(pre_mid, d_mid) * mid_scale[residual_block_index]).astype(
            jnp.bfloat16
        )
        d_pad = padded_2(d_hidden, (("seq", 0),), dilation)
        dilated_weight_gradients[residual_block_index] = (own_first(padded.T), shifted_taps(d_hidden, dilation))
        mixing_weight_gradients[residual_block_index] = (own_first(cot_here.T), middle)
        block_pairs = [dilated_weight_gradients[residual_block_index], mixing_weight_gradients[residual_block_index]]
        tiles = padded.shape[1] // (row_tile * lax.axis_size("core"))
        partner_rows = weight_gradient_buffer(block_pairs, inverse_square_root, tiles, tiles, None, row_tile)
        d_pad, partner_rows = lax.optimization_barrier((d_pad, partner_rows))
        partners[residual_block_index] = lax.ppermute(partner_rows, "core", [(0, 1), (1, 0)])
        d_act = conv_backward(d_pad, gathered, residual_block_index, c2, dilation, row_count)
        upstream_gradient = (
            upstream_gradient + gelu_back(pre_in, d_act) * in_scale[residual_block_index]
        )
    paired = None
    for b in reversed(range(residual_block_count)):
        paired = weight_gradient_buffer(
            [dilated_weight_gradients[b], mixing_weight_gradients[b]],
            inverse_square_root,
            0,
            tiles,
            partners[b],
            row_tile,
            b,
            paired,
            residual_block_count,
        )
    summed = lax.psum_scatter(paired, ("seq", "y"), scatter_dimension=0, tiled=True).astype(jnp.float32)
    own_rows = summed.shape[0]
    taps, c2 = w_dilated.shape[2], w_dilated.shape[3]
    per_block = summed.reshape(own_rows, residual_block_count, (taps + 1) * c2).transpose(1, 0, 2)
    return (
        output[None],
        upstream_gradient[None],
        per_block[:, :, : taps * c2].reshape(residual_block_count, own_rows, taps, c2),
        per_block[:, :, taps * c2 :],
    )


def solution(mesh):
    win = mesh.shape["win"]
    grid = jax.sharding.Mesh(mesh.devices.reshape(mesh.shape["seq"], win // 2, 2), ALL)
    in_specs = (
        P(WIN, "seq", None),
        P(WIN, "seq", None),
        P(None, ALL, None, None),
        P(None, ALL, None),
        P(),
        P(),
        P(),
        P(),
    )
    out_specs = (
        P(WIN, "seq", None),
        P(WIN, "seq", None),
        P(None, ALL, None, None),
        P(None, ALL, None),
    )
    return jax.shard_map(
        per_device, mesh=grid, in_specs=in_specs, out_specs=out_specs, check_vma=False
    )
```

```python
import math

import jax
import jax.numpy as jnp
from jax import lax
from jax.experimental import pallas as pl
from jax.sharding import PartitionSpec as P

dilation_steps = (8, 16)
WIN = ("y", "core")
ALL = ("seq", "y", "core")


def padded_2(block, sides, width):
    for axis, dim in sides:
        count = lax.axis_size(axis)
        forward = [(i, i + 1) for i in range(count - 1)]
        backward = [(target, source) for source, target in forward]
        low = lax.ppermute(
            lax.slice_in_dim(block, block.shape[dim] - width, None, axis=dim), axis, forward
        )
        high = lax.ppermute(lax.slice_in_dim(block, 0, width, axis=dim), axis, backward)
        block = jnp.concatenate([low, block, high], axis=dim)
    return block


def gelu_value(values):
    return jax.nn.gelu(values, approximate=True)


def gelu_back(pre_values, upstream_gradient):
    return jax.vjp(gelu_value, pre_values)[1](upstream_gradient)[0]


def conv_forward_kernel(dilation, out_rows, act_ref, w_ref, scale_ref, shift_ref, out_ref):
    tap = pl.program_id(0)
    for kernel_tap in range(3):

        @pl.when(tap == kernel_tap)
        def _():
            lower = kernel_tap * dilation
            term = jnp.dot(
                act_ref[lower : lower + out_rows, :], w_ref[...], preferred_element_type=jnp.float32
            )
            if kernel_tap == 0:
                out_ref[...] = term
            elif kernel_tap == 1:
                out_ref[...] = out_ref[...] + term
            else:
                out_ref[...] = (out_ref[...] + term) * scale_ref[...] + shift_ref[...]


def conv_backward_kernel(dilation, out_rows, grad_ref, w_ref, out_ref):
    tap = pl.program_id(0)
    numbers = (((1,), (1,)), ((), ()))
    for kernel_tap in range(3):

        @pl.when(tap == kernel_tap)
        def _():
            lower = (2 - kernel_tap) * dilation
            term = lax.dot_general(
                grad_ref[lower : lower + out_rows, :],
                w_ref[...],
                numbers,
                preferred_element_type=jnp.float32,
            )
            if kernel_tap == 0:
                out_ref[...] = term
            else:
                out_ref[...] = out_ref[...] + term


def conv_forward(padded, gathered, block, c2, scale, shift, dilation, out_rows):
    rows = gathered.shape[0]
    return pl.pallas_call(
        lambda *refs: conv_forward_kernel(dilation, out_rows, *refs),
        grid=(3,),
        in_specs=[
            pl.BlockSpec(padded.shape, lambda k: (0, 0)),
            pl.BlockSpec((rows, c2), lambda k: (0, 3 * block + k)),
            pl.BlockSpec((1, c2), lambda k: (0, 0)),
            pl.BlockSpec((1, c2), lambda k: (0, 0)),
        ],
        out_specs=pl.BlockSpec((out_rows, c2), lambda k: (0, 0)),
        out_shape=jax.ShapeDtypeStruct((out_rows, c2), jnp.float32),
    )(padded, gathered, scale.reshape(1, c2), shift.reshape(1, c2))


def conv_backward(d_pad, gathered, block, c2, dilation, out_rows):
    rows = gathered.shape[0]
    return pl.pallas_call(
        lambda *refs: conv_backward_kernel(dilation, out_rows, *refs),
        grid=(3,),
        in_specs=[
            pl.BlockSpec(d_pad.shape, lambda k: (0, 0)),
            pl.BlockSpec((rows, c2), lambda k: (0, 3 * block + k)),
        ],
        out_specs=pl.BlockSpec((out_rows, rows), lambda k: (0, 0)),
        out_shape=jax.ShapeDtypeStruct((out_rows, rows), jnp.float32),
    )(d_pad, gathered)


def fetch_weights(w_dilated, w_mix):
    blocks, rows, taps, c2 = w_dilated.shape
    local = jnp.concatenate(
        [w_dilated.reshape(blocks, rows, taps * c2).transpose(1, 0, 2).reshape(rows, -1),
         w_mix.transpose(1, 0, 2).reshape(rows, -1)],
        axis=1,
    )
    gathered = lax.all_gather(local, ALL, axis=0, tiled=True)
    split = blocks * taps * c2
    return gathered, [gathered[:, split + b * c2 : split + (b + 1) * c2] for b in range(blocks)]


def shifted_taps(d_hidden, dilation):
    return jnp.concatenate(
        [jnp.pad(d_hidden, ((k * dilation, (2 - k) * dilation), (0, 0))) for k in range(3)], axis=1
    )


def gradient_kernel(scale, layout, count, has_partner, *refs):
    out_ref = refs[-1]
    partner_ref = refs[2 * count] if has_partner else None
    for pair, (start, width) in enumerate(layout):
        lhs = refs[2 * pair][...]
        rhs = refs[2 * pair + 1][...]
        term = (jnp.dot(lhs, rhs, preferred_element_type=jnp.float32) * scale).astype(out_ref.dtype)
        if has_partner:
            term = (
                term.astype(jnp.float32) + partner_ref[:, start : start + width].astype(jnp.float32)
            ).astype(out_ref.dtype)
        out_ref[:, start : start + width] = term


def weight_gradient_buffer(
    pairs, inverse_square_root, first_tile, tiles, partner=None, row_tile=256, column_block=0, into=None, blocks=1
):
    layout = []
    start = 0
    for _, rhs in pairs:
        layout.append((start, rhs.shape[1]))
        start += rhs.shape[1]
    in_specs = []
    operands = []
    for lhs, rhs in pairs:
        in_specs.append(pl.BlockSpec((row_tile, lhs.shape[1]), lambda i: (i + first_tile, 0)))
        in_specs.append(pl.BlockSpec(rhs.shape, lambda i: (0, 0)))
        operands += [lhs, rhs]
    if partner is not None:
        in_specs.append(pl.BlockSpec((row_tile, start), lambda i: (i, 0)))
        operands.append(partner)
    aliases = {}
    if into is not None:
        in_specs.append(pl.BlockSpec(memory_space=pl.ANY))
        operands.append(into)
        aliases = {len(operands) - 1: 0}
    return pl.pallas_call(
        lambda *refs: gradient_kernel(inverse_square_root, tuple(layout), len(pairs), partner is not None, *refs),
        grid=(tiles,),
        in_specs=in_specs,
        out_specs=pl.BlockSpec((row_tile, start), lambda i: (i, column_block)),
        out_shape=jax.ShapeDtypeStruct((tiles * row_tile, blocks * start), jnp.bfloat16),
        input_output_aliases=aliases,
    )(*operands)


def own_first(rows_by_channel):
    cores = lax.axis_size("core")
    core = lax.axis_index("core")
    grouped = rows_by_channel.reshape(-1, cores, rows_by_channel.shape[0] // (cores * lax.axis_size(("seq", "y"))), rows_by_channel.shape[1])
    order = (core + jnp.arange(cores)) % cores
    return jnp.take(grouped, order, axis=1).transpose(1, 0, 2, 3).reshape(rows_by_channel.shape)


def per_device(inputs, cotangent, w_dilated, w_mix, in_scale, in_shift, mid_scale, mid_shift):
    x_local = inputs[0]
    cot_local = cotangent[0]
    row_count = x_local.shape[0]
    window_len = lax.axis_size("seq") * row_count
    inverse_square_root = 1.0 / math.sqrt(lax.axis_size("y") * lax.axis_size("core") * inputs.shape[0] * window_len)
    residual_block_count = len(dilation_steps)
    saved = []
    gathered, mixing_weights = fetch_weights(w_dilated, w_mix)
    c2 = w_dilated.shape[3]
    remaining = sum(dilation_steps)
    first_row = lax.axis_index("seq") * row_count
    stream = padded_2(x_local, (("seq", 0),), remaining).astype(jnp.float32)
    for residual_block_index in range(residual_block_count):
        dilation = dilation_steps[residual_block_index]
        w_out = mixing_weights[residual_block_index]
        pre_in = stream * in_scale[residual_block_index] + in_shift[residual_block_index]
        position = first_row - remaining + lax.broadcasted_iota(jnp.int32, (pre_in.shape[0], 1), 0)
        inside = (position >= 0) & (position < window_len)
        activated = jnp.where(inside, gelu_value(pre_in), 0.0).astype(jnp.bfloat16)
        out_rows = row_count + 2 * (remaining - dilation)
        pre_mid = conv_forward(
            activated,
            gathered,
            residual_block_index,
            c2,
            mid_scale[residual_block_index],
            mid_shift[residual_block_index],
            dilation,
            out_rows,
        )
        middle = gelu_value(pre_mid).astype(jnp.bfloat16)
        stream = stream[dilation : dilation + out_rows] + jnp.einsum(
            "pe,ce->pc", middle, w_out, preferred_element_type=jnp.float32
        )
        own = remaining - dilation
        saved.append(
            (
                w_out,
                pre_in[remaining : remaining + row_count],
                activated[own : own + row_count + 2 * dilation],
                pre_mid[own : own + row_count],
                middle[own : own + row_count],
            )
        )
        remaining -= dilation
    output = stream.astype(jnp.bfloat16)
    upstream_gradient = cot_local.astype(jnp.float32)
    dilated_weight_gradients = [None] * residual_block_count
    partners = [None] * residual_block_count
    row_tile = 384
    mixing_weight_gradients = [None] * residual_block_count
    for residual_block_index in reversed(range(residual_block_count)):
        dilation = dilation_steps[residual_block_index]
        w_out, pre_in, padded, pre_mid, middle = saved[residual_block_index]
        cot_here = upstream_gradient.astype(jnp.bfloat16)
        d_mid = jnp.dot(cot_here, w_out, preferred_element_type=jnp.float32)
        d_hidden = (gelu_back(pre_mid, d_mid) * mid_scale[residual_block_index]).astype(
            jnp.bfloat16
        )
        d_pad = padded_2(d_hidden, (("seq", 0),), dilation)
        dilated_weight_gradients[residual_block_index] = (own_first(padded.T), shifted_taps(d_hidden, dilation))
        mixing_weight_gradients[residual_block_index] = (own_first(cot_here.T), middle)
        block_pairs = [dilated_weight_gradients[residual_block_index], mixing_weight_gradients[residual_block_index]]
        tiles = padded.shape[1] // (row_tile * lax.axis_size("core"))
        partner_rows = weight_gradient_buffer(block_pairs, inverse_square_root, tiles, tiles, None, row_tile)
        if residual_block_index > 0:
            d_pad, partner_rows = lax.optimization_barrier((d_pad, partner_rows))
        partners[residual_block_index] = lax.ppermute(partner_rows, "core", [(0, 1), (1, 0)])
        d_act = conv_backward(d_pad, gathered, residual_block_index, c2, dilation, row_count)
        upstream_gradient = (
            upstream_gradient + gelu_back(pre_in, d_act) * in_scale[residual_block_index]
        )
    paired = None
    for b in reversed(range(residual_block_count)):
        paired = weight_gradient_buffer(
            [dilated_weight_gradients[b], mixing_weight_gradients[b]],
            inverse_square_root,
            0,
            tiles,
            partners[b],
            row_tile,
            b,
            paired,
            residual_block_count,
        )
    summed = lax.psum_scatter(paired, ("seq", "y"), scatter_dimension=0, tiled=True).astype(jnp.float32)
    own_rows = summed.shape[0]
    taps, c2 = w_dilated.shape[2], w_dilated.shape[3]
    per_block = summed.reshape(own_rows, residual_block_count, (taps + 1) * c2).transpose(1, 0, 2)
    return (
        output[None],
        upstream_gradient[None],
        per_block[:, :, : taps * c2].reshape(residual_block_count, own_rows, taps, c2),
        per_block[:, :, taps * c2 :],
    )


def solution(mesh):
    win = mesh.shape["win"]
    grid = jax.sharding.Mesh(mesh.devices.reshape(mesh.shape["seq"], win // 2, 2), ALL)
    in_specs = (
        P(WIN, "seq", None),
        P(WIN, "seq", None),
        P(None, ALL, None, None),
        P(None, ALL, None),
        P(),
        P(),
        P(),
        P(),
    )
    out_specs = (
        P(WIN, "seq", None),
        P(WIN, "seq", None),
        P(None, ALL, None, None),
        P(None, ALL, None),
    )
    return jax.shard_map(
        per_device, mesh=grid, in_specs=in_specs, out_specs=out_specs, check_vma=False
    )
```

```python
import math

import jax
import jax.numpy as jnp
from jax import lax
from jax.experimental import pallas as pl
from jax.sharding import PartitionSpec as P

dilation_steps = (8, 16)
WIN = ("y", "core")
ALL = ("seq", "y", "core")


def padded_2(block, sides, width):
    for axis, dim in sides:
        count = lax.axis_size(axis)
        forward = [(i, i + 1) for i in range(count - 1)]
        backward = [(target, source) for source, target in forward]
        low = lax.ppermute(
            lax.slice_in_dim(block, block.shape[dim] - width, None, axis=dim), axis, forward
        )
        high = lax.ppermute(lax.slice_in_dim(block, 0, width, axis=dim), axis, backward)
        block = jnp.concatenate([low, block, high], axis=dim)
    return block


def gelu_value(values):
    return jax.nn.gelu(values, approximate=True)


def gelu_back(pre_values, upstream_gradient):
    return jax.vjp(gelu_value, pre_values)[1](upstream_gradient)[0]


def conv_forward_kernel(dilation, out_rows, act_ref, w_ref, scale_ref, shift_ref, out_ref, mid_ref):
    tap = pl.program_id(0)
    for kernel_tap in range(3):

        @pl.when(tap == kernel_tap)
        def _():
            lower = kernel_tap * dilation
            term = jnp.dot(
                act_ref[lower : lower + out_rows, :], w_ref[...], preferred_element_type=jnp.float32
            )
            if kernel_tap == 0:
                out_ref[...] = term
            elif kernel_tap == 1:
                out_ref[...] = out_ref[...] + term
            else:
                pre = (out_ref[...] + term) * scale_ref[...] + shift_ref[...]
                out_ref[...] = pre
                mid_ref[...] = gelu_value(pre).astype(mid_ref.dtype)


def conv_backward_kernel(dilation, out_rows, grad_ref, w_ref, out_ref):
    tap = pl.program_id(0)
    numbers = (((1,), (1,)), ((), ()))
    for kernel_tap in range(3):

        @pl.when(tap == kernel_tap)
        def _():
            lower = (2 - kernel_tap) * dilation
            term = lax.dot_general(
                grad_ref[lower : lower + out_rows, :],
                w_ref[...],
                numbers,
                preferred_element_type=jnp.float32,
            )
            if kernel_tap == 0:
                out_ref[...] = term
            else:
                out_ref[...] = out_ref[...] + term


def conv_forward(padded, gathered, block, c2, scale, shift, dilation, out_rows):
    rows = gathered.shape[0]
    return pl.pallas_call(
        lambda *refs: conv_forward_kernel(dilation, out_rows, *refs),
        grid=(3,),
        in_specs=[
            pl.BlockSpec(padded.shape, lambda k: (0, 0)),
            pl.BlockSpec((rows, c2), lambda k: (0, 3 * block + k)),
            pl.BlockSpec((1, c2), lambda k: (0, 0)),
            pl.BlockSpec((1, c2), lambda k: (0, 0)),
        ],
        out_specs=[pl.BlockSpec((out_rows, c2), lambda k: (0, 0))] * 2,
        out_shape=[
            jax.ShapeDtypeStruct((out_rows, c2), jnp.float32),
            jax.ShapeDtypeStruct((out_rows, c2), jnp.bfloat16),
        ],
    )(padded, gathered, scale.reshape(1, c2), shift.reshape(1, c2))


def conv_backward(d_pad, gathered, block, c2, dilation, out_rows):
    rows = gathered.shape[0]
    return pl.pallas_call(
        lambda *refs: conv_backward_kernel(dilation, out_rows, *refs),
        grid=(3,),
        in_specs=[
            pl.BlockSpec(d_pad.shape, lambda k: (0, 0)),
            pl.BlockSpec((rows, c2), lambda k: (0, 3 * block + k)),
        ],
        out_specs=pl.BlockSpec((out_rows, rows), lambda k: (0, 0)),
        out_shape=jax.ShapeDtypeStruct((out_rows, rows), jnp.float32),
    )(d_pad, gathered)


def fetch_weights(w_dilated, w_mix):
    blocks, rows, taps, c2 = w_dilated.shape
    local = jnp.concatenate(
        [w_dilated.reshape(blocks, rows, taps * c2).transpose(1, 0, 2).reshape(rows, -1),
         w_mix.transpose(1, 0, 2).reshape(rows, -1)],
        axis=1,
    )
    gathered = lax.all_gather(local, ALL, axis=0, tiled=True)
    split = blocks * taps * c2
    return gathered, [gathered[:, split + b * c2 : split + (b + 1) * c2] for b in range(blocks)]


def shifted_taps(d_hidden, dilation):
    return jnp.concatenate(
        [jnp.pad(d_hidden, ((k * dilation, (2 - k) * dilation), (0, 0))) for k in range(3)], axis=1
    )


def gradient_kernel(scale, layout, count, has_partner, *refs):
    out_ref = refs[-1]
    partner_ref = refs[2 * count] if has_partner else None
    for pair, (start, width) in enumerate(layout):
        lhs = refs[2 * pair][...]
        rhs = refs[2 * pair + 1][...]
        term = (jnp.dot(lhs, rhs, preferred_element_type=jnp.float32) * scale).astype(out_ref.dtype)
        if has_partner:
            term = (
                term.astype(jnp.float32) + partner_ref[:, start : start + width].astype(jnp.float32)
            ).astype(out_ref.dtype)
        out_ref[:, start : start + width] = term


def weight_gradient_buffer(
    pairs, inverse_square_root, first_tile, tiles, partner=None, row_tile=256, column_block=0, into=None, blocks=1
):
    layout = []
    start = 0
    for _, rhs in pairs:
        layout.append((start, rhs.shape[1]))
        start += rhs.shape[1]
    in_specs = []
    operands = []
    for lhs, rhs in pairs:
        in_specs.append(pl.BlockSpec((row_tile, lhs.shape[1]), lambda i: (i + first_tile, 0)))
        in_specs.append(pl.BlockSpec(rhs.shape, lambda i: (0, 0)))
        operands += [lhs, rhs]
    if partner is not None:
        in_specs.append(pl.BlockSpec((row_tile, start), lambda i: (i, 0)))
        operands.append(partner)
    aliases = {}
    if into is not None:
        in_specs.append(pl.BlockSpec(memory_space=pl.ANY))
        operands.append(into)
        aliases = {len(operands) - 1: 0}
    return pl.pallas_call(
        lambda *refs: gradient_kernel(inverse_square_root, tuple(layout), len(pairs), partner is not None, *refs),
        grid=(tiles,),
        in_specs=in_specs,
        out_specs=pl.BlockSpec((row_tile, start), lambda i: (i, column_block)),
        out_shape=jax.ShapeDtypeStruct((tiles * row_tile, blocks * start), jnp.bfloat16),
        input_output_aliases=aliases,
    )(*operands)


def own_first(rows_by_channel):
    cores = lax.axis_size("core")
    core = lax.axis_index("core")
    grouped = rows_by_channel.reshape(-1, cores, rows_by_channel.shape[0] // (cores * lax.axis_size(("seq", "y"))), rows_by_channel.shape[1])
    order = (core + jnp.arange(cores)) % cores
    return jnp.take(grouped, order, axis=1).transpose(1, 0, 2, 3).reshape(rows_by_channel.shape)


def per_device(inputs, cotangent, w_dilated, w_mix, in_scale, in_shift, mid_scale, mid_shift):
    x_local = inputs[0]
    cot_local = cotangent[0]
    row_count = x_local.shape[0]
    window_len = lax.axis_size("seq") * row_count
    inverse_square_root = 1.0 / math.sqrt(lax.axis_size("y") * lax.axis_size("core") * inputs.shape[0] * window_len)
    residual_block_count = len(dilation_steps)
    saved = []
    gathered, mixing_weights = fetch_weights(w_dilated, w_mix)
    c2 = w_dilated.shape[3]
    remaining = sum(dilation_steps)
    first_row = lax.axis_index("seq") * row_count
    stream = padded_2(x_local, (("seq", 0),), remaining).astype(jnp.float32)
    for residual_block_index in range(residual_block_count):
        dilation = dilation_steps[residual_block_index]
        w_out = mixing_weights[residual_block_index]
        pre_in = stream * in_scale[residual_block_index] + in_shift[residual_block_index]
        position = first_row - remaining + lax.broadcasted_iota(jnp.int32, (pre_in.shape[0], 1), 0)
        inside = (position >= 0) & (position < window_len)
        activated = jnp.where(inside, gelu_value(pre_in), 0.0).astype(jnp.bfloat16)
        out_rows = row_count + 2 * (remaining - dilation)
        pre_mid, middle = conv_forward(
            activated,
            gathered,
            residual_block_index,
            c2,
            mid_scale[residual_block_index],
            mid_shift[residual_block_index],
            dilation,
            out_rows,
        )
        stream = stream[dilation : dilation + out_rows] + jnp.einsum(
            "pe,ce->pc", middle, w_out, preferred_element_type=jnp.float32
        )
        own = remaining - dilation
        saved.append(
            (
                w_out,
                pre_in[remaining : remaining + row_count],
                activated[own : own + row_count + 2 * dilation],
                pre_mid[own : own + row_count],
                middle[own : own + row_count],
            )
        )
        remaining -= dilation
    output = stream.astype(jnp.bfloat16)
    upstream_gradient = cot_local.astype(jnp.float32)
    dilated_weight_gradients = [None] * residual_block_count
    partners = [None] * residual_block_count
    row_tile = 384
    mixing_weight_gradients = [None] * residual_block_count
    for residual_block_index in reversed(range(residual_block_count)):
        dilation = dilation_steps[residual_block_index]
        w_out, pre_in, padded, pre_mid, middle = saved[residual_block_index]
        cot_here = upstream_gradient.astype(jnp.bfloat16)
        d_mid = jnp.dot(cot_here, w_out, preferred_element_type=jnp.float32)
        d_hidden = (gelu_back(pre_mid, d_mid) * mid_scale[residual_block_index]).astype(
            jnp.bfloat16
        )
        d_pad = padded_2(d_hidden, (("seq", 0),), dilation)
        dilated_weight_gradients[residual_block_index] = (own_first(padded.T), shifted_taps(d_hidden, dilation))
        mixing_weight_gradients[residual_block_index] = (own_first(cot_here.T), middle)
        block_pairs = [dilated_weight_gradients[residual_block_index], mixing_weight_gradients[residual_block_index]]
        tiles = padded.shape[1] // (row_tile * lax.axis_size("core"))
        partner_rows = weight_gradient_buffer(block_pairs, inverse_square_root, tiles, tiles, None, row_tile)
        if residual_block_index > 0:
            d_pad, partner_rows = lax.optimization_barrier((d_pad, partner_rows))
        partners[residual_block_index] = lax.ppermute(partner_rows, "core", [(0, 1), (1, 0)])
        d_act = conv_backward(d_pad, gathered, residual_block_index, c2, dilation, row_count)
        upstream_gradient = (
            upstream_gradient + gelu_back(pre_in, d_act) * in_scale[residual_block_index]
        )
    paired = None
    for b in reversed(range(residual_block_count)):
        paired = weight_gradient_buffer(
            [dilated_weight_gradients[b], mixing_weight_gradients[b]],
            inverse_square_root,
            0,
            tiles,
            partners[b],
            row_tile,
            b,
            paired,
            residual_block_count,
        )
    summed = lax.psum_scatter(paired, ("seq", "y"), scatter_dimension=0, tiled=True).astype(jnp.float32)
    own_rows = summed.shape[0]
    taps, c2 = w_dilated.shape[2], w_dilated.shape[3]
    per_block = summed.reshape(own_rows, residual_block_count, (taps + 1) * c2).transpose(1, 0, 2)
    return (
        output[None],
        upstream_gradient[None],
        per_block[:, :, : taps * c2].reshape(residual_block_count, own_rows, taps, c2),
        per_block[:, :, taps * c2 :],
    )


def solution(mesh):
    win = mesh.shape["win"]
    grid = jax.sharding.Mesh(mesh.devices.reshape(mesh.shape["seq"], win // 2, 2), ALL)
    in_specs = (
        P(WIN, "seq", None),
        P(WIN, "seq", None),
        P(None, ALL, None, None),
        P(None, ALL, None),
        P(),
        P(),
        P(),
        P(),
    )
    out_specs = (
        P(WIN, "seq", None),
        P(WIN, "seq", None),
        P(None, ALL, None, None),
        P(None, ALL, None),
    )
    return jax.shard_map(
        per_device, mesh=grid, in_specs=in_specs, out_specs=out_specs, check_vma=False
    )
```
